128 devices in a mesh: dp: 4 (over z_hi, core), mp: 32 (over x, y, z_lo).
Axes of the slice: x: 4, y: 4, z: 4 (z_hi: 2, z_lo: 2; z = z_hi * 2 + z_lo), core: 2. Of those that a mesh axis runs over, the one named last changes fastest.
Arguments:
- residual_input: bfloat16 [2048, 4608], P(('dp', 'mp')), may hold values from -6 to 6
- before_attention_gain: float32 [4608], replicated, may hold values from 0.25 to 1.75
- after_attention_gain: float32 [4608], replicated, may hold values from 0.25 to 1.75
- before_feedforward_gain: float32 [4608], replicated, may hold values from 0.25 to 1.75
- after_feedforward_gain: float32 [4608], replicated, may hold values from 0.25 to 1.75
- query_weight: bfloat16 [4608, 4096], P(None, 'mp'), may hold values from -0.09375 to 0.09375
- key_value_weight: bfloat16 [4608, 2, 32, 128], P(None, None, 'mp'), as said below
- output_weight: bfloat16 [4096, 4608], P('mp'), may hold values from -0.09375 to 0.09375
- gate_matrix: bfloat16 [4608, 20480], P(None, 'mp'), may hold values from -0.09375 to 0.09375
- up_matrix: bfloat16 [4608, 20480], P(None, 'mp'), may hold values from -0.09375 to 0.09375
- down_matrix: bfloat16 [20480, 4608], P('mp'), may hold values from -0.0390625 to 0.0390625
- key_value_cache: bfloat16 [256, 2, 32, 16, 128], P('dp', None, 'mp'), as said below
- projected_lowrank_left: bfloat16 [64, 4608, 16], P('mp'), may hold values from -0.09375 to 0.09375
- projected_lowrank_right: bfloat16 [64, 16, 3, 32, 128], P(None, None, None, 'mp'), as said below
- result_lowrank_left: bfloat16 [64, 4096, 16], P(None, 'mp'), may hold values from -0.09375 to 0.09375
- result_lowrank_right: bfloat16 [64, 16, 4608], P('mp'), may hold values from -1.5 to 1.5
- token_request: int32 [4, 512], P('dp'), may hold values from 0 to 7, never falling along the last dimension, each value on 1 to 256 neighbouring positions
- lowrank_choice_by_prompt: int32 [4, 8], P('dp'), may hold values from 0 to 63
- adapter_position: int32 [64], replicated, may hold values from 0 to 63, each once
- request_pages: int32 [4, 8, 4], replicated, may hold values from 0 to 255
Outputs:
- hidden_out: bfloat16 [2048, 4608], P(('dp', 'mp'))
- kv_new: bfloat16 [2048, 2, 32, 128], P('dp', None, 'mp')
The draws below stay inside these ranges and needn't reach their ends.
Inputs may be any that keep to these rules, and one draw needn't show every extreme that they name: `key_value_weight`: query heads h and h2 with h // 2 == h2 // 2 have equal key and value weights: they share one key and value head. `key_value_cache`: query heads that share a key and value head have equal cached keys and values. `projected_lowrank_right`: the key and value parts of query heads that share a key and value head are equal. `token_request`: numbers never fall along a group; every request has at least one token. `adapter_position`: each slot once. `request_pages`: pages may repeat within and across requests.
All inputs are finite; a program needn't handle non-finite values.
Results may differ from the reference program's by a relative error of at most 0.035.
Values may be sent and summed in bfloat16 or wider, within the bound.
No kernel may reach another device: no remote copies, remote signals or barrier semaphores. Data moves between devices by JAX's collectives and lax.ppermute only.
A program may use at most 128 MiB of HBM per device.

```python
import math
import jax
import jax.numpy as jnp
import numpy as np
from jax import lax

HIDDEN_BREADTH = 4608
ASKING_CHANNELS = 32
PAIR_CHANNELS = 16
CHANNEL_LENGTH = 128
FF = 20480
NUM_LOW_TERMS = 64
LOW_DIMENSION = 16
SHARD_PROMPT_LEN = 512
SHARD_PROMPTS = 8
PPR = 4
PAGE = 16
PROMPT_LEN_ALL = 2048
POOL = 256
N_DP = 4
N_MP = 32


def common_channels(key, dims_shape, head_axis, spread):
    drawn = jax.random.normal(key, dims_shape, jnp.float32) * spread
    return jnp.repeat(drawn, ASKING_CHANNELS // PAIR_CHANNELS, axis=head_axis)


def draw_key_value_weight(key, part):
    return common_channels(jax.random.fold_in(key, 11), (HIDDEN_BREADTH, 2, PAIR_CHANNELS, CHANNEL_LENGTH), 2, HIDDEN_BREADTH ** (-0.5)).astype(jnp.bfloat16)


def draw_key_value_cache(key, part):
    return common_channels(jax.random.fold_in(key, 12), (POOL, 2, PAIR_CHANNELS, PAGE, CHANNEL_LENGTH), 2, 1.0).astype(jnp.bfloat16)


def draw_projected_lowrank_right(key, part):
    asking_share = jax.random.normal(jax.random.fold_in(key, 13), (NUM_LOW_TERMS, LOW_DIMENSION, 1, ASKING_CHANNELS, CHANNEL_LENGTH), jnp.float32) * LOW_DIMENSION ** (-0.5)
    common_share = common_channels(jax.random.fold_in(key, 14), (NUM_LOW_TERMS, LOW_DIMENSION, 2, PAIR_CHANNELS, CHANNEL_LENGTH), 3, LOW_DIMENSION ** (-0.5))
    return jnp.concatenate([asking_share, common_share], axis=2).astype(jnp.bfloat16)


def touch_ends(values, own_key, least, high):
    spot = [jax.random.randint(jax.random.fold_in(own_key, axis), (), 0, length) for axis, length in enumerate(values.shape)]
    main_axis = values.shape.index(max(values.shape))
    beside = spot[:main_axis] + [(spot[main_axis] + 1) % values.shape[main_axis]] + spot[main_axis + 1:]
    return values.at[tuple(spot)].set(least).at[tuple(beside)].set(high)


def level_of(stream_key, dims, shards, smallest, top_value):
    level, own = 1.0, jax.random.fold_in(stream_key, 6)
    for axis_at, parts in shards:
        heights = jnp.exp(jax.random.uniform(jax.random.fold_in(own, axis_at), (parts,), jnp.float32, smallest / len(shards), top_value / len(shards)))
        level = level * jnp.repeat(heights, dims[axis_at] // parts).reshape([-1 if axis == axis_at else 1 for axis in range(len(dims))])
    return level


def cumulative_ranks(amount, lean):
    portions = [(1 << 20) // math.isqrt(rank ** lean) + 1 for rank in range(1, amount + 1)]
    width = 1 + sum(portions) // (1 << 30)
    return np.cumsum(np.array([max(1, weight // width) for weight in portions]))


def ranked(own_key, shape, count, skew):
    listing = cumulative_ranks(count, skew)
    ticket = jax.random.randint(jax.random.fold_in(own_key, 1), shape, 0, int(listing[count - 1]))
    standing = jnp.searchsorted(jnp.asarray(listing, jnp.int32), ticket, side="right")
    return jax.random.permutation(jax.random.fold_in(own_key, 2), count)[standing].astype(jnp.int32)


def split_up(count, total, limit, slope):
    weights = [(1 << 20) // math.isqrt(standing ** slope) + 1 for standing in range(2, count + 1)]
    spare, holding = total - limit - (count - 1), [1] * (count - 1)
    while spare > 0:
        candidates = [i for i in range(count - 1) if holding[i] < limit]
        whole, budget = sum([weights[i] for i in candidates]), spare
        for i in candidates:
            more = min(limit - holding[i], max(1, budget * weights[i] // whole), spare)
            holding[i] = holding[i] + more
            spare = spare - more
    return np.array([limit] + holding)


def uneven(own_key, number_of, total, reach, skew):
    if number_of == 2:
        one = jax.random.randint(own_key, (), max(1, total - reach), min(reach, total - 1) + 1)
        return jnp.stack([one, total - one])
    sizes = jnp.asarray(split_up(number_of, total, reach, skew), jnp.int32)
    couples = (number_of - 1) // 2
    donor, taker = sizes[1:1 + 2 * couples:2], sizes[2:2 + 2 * couples:2]
    room = jnp.minimum(donor - 1, reach - taker)
    shifted = jax.random.randint(jax.random.fold_in(own_key, 1), (couples,), 0, 1 << 20) % (room + 1)
    sizes = sizes.at[1:1 + 2 * couples:2].set(donor - shifted).at[2:2 + 2 * couples:2].set(taker + shifted)
    return sizes[jax.random.permutation(jax.random.fold_in(own_key, 2), number_of)]


def gaussian(key, extent, scale, bound, split=(), held_as=jnp.bfloat16):
    array = scale * jax.random.normal(key, extent, jnp.float32)
    if split:
        array = array * level_of(key, extent, split, -0.22, 0.18)
    return jnp.clip(array, -bound, bound).astype(held_as)


def setup_inputs(seed: int = 0) -> dict:
    key_of = jax.random.split(jax.random.key(seed), 21)
    residual_input = gaussian(key_of[0], (PROMPT_LEN_ALL, HIDDEN_BREADTH), 1.0, 6.0, ((0, 128),))
    before_attention_gain = jnp.clip(1.0 + 0.15 * jax.random.normal(key_of[1], (HIDDEN_BREADTH,), jnp.float32), 0.25, 1.75)
    after_attention_gain = jnp.clip(1.0 + 0.15 * jax.random.normal(key_of[2], (HIDDEN_BREADTH,), jnp.float32), 0.25, 1.75)
    before_feedforward_gain = jnp.clip(1.0 + 0.15 * jax.random.normal(key_of[3], (HIDDEN_BREADTH,), jnp.float32), 0.25, 1.75)
    after_feedforward_gain = jnp.clip(1.0 + 0.15 * jax.random.normal(key_of[4], (HIDDEN_BREADTH,), jnp.float32), 0.25, 1.75)
    query_weight = gaussian(key_of[5], (HIDDEN_BREADTH, ASKING_CHANNELS * CHANNEL_LENGTH), HIDDEN_BREADTH ** -0.5, 0.09375, ((1, 32),))
    key_value_weight = draw_key_value_weight(jax.random.fold_in(key_of[20], 71), 0)
    output_weight = gaussian(key_of[7], (ASKING_CHANNELS * CHANNEL_LENGTH, HIDDEN_BREADTH), (ASKING_CHANNELS * CHANNEL_LENGTH) ** -0.5, 0.09375, ((0, 32),))
    gate_matrix = gaussian(key_of[8], (HIDDEN_BREADTH, FF), HIDDEN_BREADTH ** -0.5, 0.09375, ((1, 32),))
    up_matrix = gaussian(key_of[9], (HIDDEN_BREADTH, FF), HIDDEN_BREADTH ** -0.5, 0.09375, ((1, 32),))
    down_matrix = gaussian(key_of[10], (FF, HIDDEN_BREADTH), FF ** -0.5, 0.0390625, ((0, 32),))
    key_value_cache = draw_key_value_cache(jax.random.fold_in(key_of[20], 71), 0)
    projected_lowrank_left = gaussian(key_of[12], (NUM_LOW_TERMS, HIDDEN_BREADTH, LOW_DIMENSION), HIDDEN_BREADTH ** -0.5, 0.09375, ((0, 32),))
    projected_lowrank_right = draw_projected_lowrank_right(jax.random.fold_in(key_of[20], 71), 0)
    result_lowrank_left = gaussian(key_of[14], (NUM_LOW_TERMS, ASKING_CHANNELS * CHANNEL_LENGTH, LOW_DIMENSION), (ASKING_CHANNELS * CHANNEL_LENGTH) ** -0.5, 0.09375, ((1, 32),))
    result_lowrank_right = gaussian(key_of[15], (NUM_LOW_TERMS, LOW_DIMENSION, HIDDEN_BREADTH), LOW_DIMENSION ** -0.5, 1.5, ((0, 32),))
    token_request = jax.vmap(lambda own: jnp.searchsorted(jnp.cumsum(uneven(own, SHARD_PROMPTS, SHARD_PROMPT_LEN, SHARD_PROMPT_LEN // 2, 2)), jnp.arange(SHARD_PROMPT_LEN), side="right"))(jax.random.split(key_of[16], N_DP)).reshape((N_DP, SHARD_PROMPT_LEN)).astype(jnp.int32)
    lowrank_choice_by_prompt = touch_ends(ranked(key_of[17], (N_DP, SHARD_PROMPTS), NUM_LOW_TERMS, 2), jax.random.fold_in(key_of[17], 3), 0, NUM_LOW_TERMS - 1).astype(jnp.int32)
    adapter_position = jax.random.permutation(key_of[18], NUM_LOW_TERMS).astype(jnp.int32)
    request_pages = touch_ends(jax.random.randint(key_of[19], (N_DP, SHARD_PROMPTS, PPR), 0, POOL), jax.random.fold_in(key_of[19], 1), 0, POOL - 1).astype(jnp.int32)
    return {"residual_input": residual_input, "before_attention_gain": before_attention_gain, "after_attention_gain": after_attention_gain, "before_feedforward_gain": before_feedforward_gain, "after_feedforward_gain": after_feedforward_gain, "query_weight": query_weight, "key_value_weight": key_value_weight, "output_weight": output_weight, "gate_matrix": gate_matrix, "up_matrix": up_matrix, "down_matrix": down_matrix, "key_value_cache": key_value_cache, "projected_lowrank_left": projected_lowrank_left, "projected_lowrank_right": projected_lowrank_right, "result_lowrank_left": result_lowrank_left, "result_lowrank_right": result_lowrank_right, "token_request": token_request, "lowrank_choice_by_prompt": lowrank_choice_by_prompt, "adapter_position": adapter_position, "request_pages": request_pages}


EPS = 1e-06
SOFTCAP = 50.0

def rms_scale(values, scaling):
    mean_square = lax.optimization_barrier(jnp.mean(values * values, axis=-1, keepdims=True))
    return values * lax.rsqrt(mean_square + EPS) * scaling.astype(jnp.float32)

def apply_rotary(values, token_positions):
    half_dim = values.shape[-1] // 2
    frequency = 10000.0 ** (-2.0 * jnp.arange(half_dim, dtype=jnp.float32) / values.shape[-1])
    angles = token_positions.astype(jnp.float32)[:, None] * frequency[None, :]
    cosine = jnp.cos(angles)[:, None, :]
    sine_part = jnp.sin(angles)[:, None, :]
    first_half = values[..., :half_dim]
    second_half = values[..., half_dim:]
    return jnp.concatenate([first_half * cosine - second_half * sine_part, second_half * cosine + first_half * sine_part], axis=-1)

def positions_of(segments):
    length = segments.shape[0]
    earlier = lax.optimization_barrier(jnp.sum((segments[None, :] < segments[:, None]).astype(jnp.int32), axis=1))
    return (PPR * PAGE + jnp.arange(length, dtype=jnp.int32) - earlier).astype(jnp.int32)

def capped(scores):
    return SOFTCAP * jnp.tanh(scores / SOFTCAP)

def attend(query_rows, keys_new, fresh_values, keys_pre, values_pre, segments):
    scale_factor = 1.0 / math.sqrt(HIDDEN_BREADTH // ASKING_CHANNELS)
    length = segments.shape[0]
    prefix_owner = jnp.arange(keys_pre.shape[1], dtype=jnp.int32) // (PPR * PAGE)
    mask_pre = (prefix_owner[None, :] == segments[:, None])[None]
    ordinal = jnp.arange(length, dtype=jnp.int32)
    mask_new = ((segments[None, :] == segments[:, None]) & (ordinal[None, :] <= ordinal[:, None]))[None]
    scores_pre = jnp.einsum('thd,hjd->htj', query_rows.astype(jnp.float32), keys_pre.astype(jnp.float32)) * scale_factor
    scores_new = jnp.einsum('thd,uhd->htu', query_rows.astype(jnp.float32), keys_new.astype(jnp.float32)) * scale_factor
    weight_pre = jnp.where(mask_pre, jnp.exp(capped(scores_pre)), 0.0)
    weight_new = jnp.where(mask_new, jnp.exp(capped(scores_new)), 0.0)
    totals = lax.optimization_barrier(jnp.sum(weight_pre, axis=-1, keepdims=True)) + lax.optimization_barrier(jnp.sum(weight_new, axis=-1, keepdims=True))
    probs_pre = (weight_pre / totals).astype(jnp.bfloat16)
    probs_new = (weight_new / totals).astype(jnp.bfloat16)
    mixture = jnp.einsum('htj,hjd->thd', probs_pre.astype(jnp.float32), values_pre.astype(jnp.float32))
    mixture = mixture + jnp.einsum('htu,uhd->thd', probs_new.astype(jnp.float32), fresh_values.astype(jnp.float32))
    return mixture.astype(jnp.bfloat16).reshape(length, -1)

def reference(residual_input, before_attention_gain, after_attention_gain, before_feedforward_gain, after_feedforward_gain, query_weight, key_value_weight, output_weight, gate_matrix, up_matrix, down_matrix, key_value_cache, projected_lowrank_left, projected_lowrank_right, result_lowrank_left, result_lowrank_right, token_request, lowrank_choice_by_prompt, adapter_position, request_pages):
    residual = residual_input.astype(jnp.float32)
    normalized_rows = rms_scale(residual, before_attention_gain).astype(jnp.bfloat16)
    query_rows = jnp.dot(normalized_rows, query_weight, preferred_element_type=jnp.float32).reshape(PROMPT_LEN_ALL, ASKING_CHANNELS, CHANNEL_LENGTH)
    key_value_rows = jnp.dot(normalized_rows, key_value_weight.reshape(HIDDEN_BREADTH, 2 * ASKING_CHANNELS * CHANNEL_LENGTH), preferred_element_type=jnp.float32).reshape(PROMPT_LEN_ALL, 2, ASKING_CHANNELS, CHANNEL_LENGTH)
    group_of = (jnp.arange(PROMPT_LEN_ALL, dtype=jnp.int32) // SHARD_PROMPT_LEN).astype(jnp.int32)
    flat_segments = token_request.reshape(PROMPT_LEN_ALL)
    token_adapter = lowrank_choice_by_prompt[group_of, flat_segments]
    token_adapter_slot = adapter_position[token_adapter]
    gathered_down = jnp.einsum('bg,wgv->bwv', normalized_rows.astype(jnp.float32), projected_lowrank_left.astype(jnp.float32))
    lowrank_source = jnp.take_along_axis(gathered_down, token_adapter_slot[:, None, None].astype(jnp.int32), axis=1)[:, 0, :].astype(jnp.bfloat16)
    request_range = jnp.arange(SHARD_PROMPTS, dtype=jnp.int32)
    adapter_pieces = []
    position_parts = []
    for shard_ordinal in range(N_DP):
        line_span = slice(shard_ordinal * SHARD_PROMPT_LEN, (shard_ordinal + 1) * SHARD_PROMPT_LEN)
        segments = token_request[shard_ordinal]
        choice_mask_table = (segments[:, None] == request_range[None, :]).astype(jnp.bfloat16)
        broadened_lines = (choice_mask_table[:, :, None] * lowrank_source[line_span][:, None, :]).reshape(SHARD_PROMPT_LEN, SHARD_PROMPTS * LOW_DIMENSION)
        raised_result_lines = projected_lowrank_right[lowrank_choice_by_prompt[shard_ordinal]].reshape(SHARD_PROMPTS * LOW_DIMENSION, 3 * ASKING_CHANNELS * CHANNEL_LENGTH)
        adapter_pieces.append(jnp.dot(broadened_lines, raised_result_lines, preferred_element_type=jnp.float32))
        position_parts.append(positions_of(segments))
    adapter_query_key_value = jnp.concatenate(adapter_pieces, axis=0).reshape(PROMPT_LEN_ALL, 3, ASKING_CHANNELS, CHANNEL_LENGTH)
    token_positions = jnp.concatenate(position_parts, axis=0)
    rotary_queries = apply_rotary(query_rows + adapter_query_key_value[:, 0], token_positions).astype(jnp.bfloat16)
    rotary_keys = apply_rotary(key_value_rows[:, 0] + adapter_query_key_value[:, 1], token_positions).astype(jnp.bfloat16)
    fresh_values = (key_value_rows[:, 1] + adapter_query_key_value[:, 2]).astype(jnp.bfloat16)
    kv_new = jnp.stack([rotary_keys, fresh_values], axis=1)
    attended_parts = []
    output_adapter_pieces = []
    for shard_ordinal in range(N_DP):
        line_span = slice(shard_ordinal * SHARD_PROMPT_LEN, (shard_ordinal + 1) * SHARD_PROMPT_LEN)
        segments = token_request[shard_ordinal]
        page_ids = request_pages[shard_ordinal].reshape(SHARD_PROMPTS * PPR)
        chosen = key_value_cache[page_ids]
        keys_pre = jnp.transpose(chosen[:, 0], (1, 0, 2, 3)).reshape(ASKING_CHANNELS, SHARD_PROMPTS * PPR * PAGE, CHANNEL_LENGTH)
        values_pre = jnp.transpose(chosen[:, 1], (1, 0, 2, 3)).reshape(ASKING_CHANNELS, SHARD_PROMPTS * PPR * PAGE, CHANNEL_LENGTH)
        attended = attend(rotary_queries[line_span], rotary_keys[line_span], fresh_values[line_span], keys_pre, values_pre, segments)
        attended_parts.append(attended)
        membership = segments[:, None] == request_range[None, :]
        down_output_rows = result_lowrank_left[lowrank_choice_by_prompt[shard_ordinal]]
        request_factors = jnp.einsum('tc,rck->trk', attended.astype(jnp.float32), down_output_rows.astype(jnp.float32))
        output_adapter_pieces.append(lax.optimization_barrier(jnp.sum(jnp.where(membership[:, :, None], request_factors, 0.0), axis=1)))
    attended_all = jnp.concatenate(attended_parts, axis=0)
    result_lowrank_source = jnp.concatenate(output_adapter_pieces, axis=0).astype(jnp.bfloat16)
    cols_dev = ASKING_CHANNELS * CHANNEL_LENGTH // N_MP
    seats_each_shard = NUM_LOW_TERMS // N_MP
    units_dev = FF // N_MP

    def attn_shard(shard_place, running):
        start_col = (shard_place * cols_dev).astype(jnp.int32)
        attn_part = lax.dynamic_slice_in_dim(attended_all, start_col, cols_dev, 1)
        weight_part = lax.dynamic_slice_in_dim(output_weight, start_col, cols_dev, 0)
        slot_ids = (shard_place * seats_each_shard + jnp.arange(seats_each_shard, dtype=jnp.int32)).astype(jnp.int32)
        resident_here = (token_adapter_slot[:, None] == slot_ids[None, :]).astype(jnp.bfloat16)
        broadened_result = (resident_here[:, :, None] * result_lowrank_source[:, None, :]).reshape(PROMPT_LEN_ALL, seats_each_shard * LOW_DIMENSION)
        raised_fragment = lax.dynamic_slice_in_dim(result_lowrank_right, (shard_place * seats_each_shard).astype(jnp.int32), seats_each_shard, 0).reshape(seats_each_shard * LOW_DIMENSION, HIDDEN_BREADTH)
        shard_sum = jnp.dot(attn_part, weight_part, preferred_element_type=jnp.float32) + jnp.dot(broadened_result, raised_fragment, preferred_element_type=jnp.float32)
        return running + lax.optimization_barrier(shard_sum.astype(jnp.bfloat16)).astype(jnp.float32)
    attn_sum = lax.fori_loop(jnp.int32(0), jnp.int32(N_MP), attn_shard, jnp.zeros((PROMPT_LEN_ALL, HIDDEN_BREADTH), jnp.float32))
    after_attn = (residual + rms_scale(attn_sum, after_attention_gain)).astype(jnp.bfloat16)
    normed_ffw = rms_scale(after_attn.astype(jnp.float32), before_feedforward_gain).astype(jnp.bfloat16)
    gated = jnp.dot(normed_ffw, gate_matrix, preferred_element_type=jnp.float32)
    upward = jnp.dot(normed_ffw, up_matrix, preferred_element_type=jnp.float32)
    hidden = (jax.nn.gelu(gated, approximate=True) * upward).astype(jnp.bfloat16)

    def ffw_shard(shard_place, running):
        start_unit = (shard_place * units_dev).astype(jnp.int32)
        hidden_part = lax.dynamic_slice_in_dim(hidden, start_unit, units_dev, 1)
        down_part = lax.dynamic_slice_in_dim(down_matrix, start_unit, units_dev, 0)
        shard_sum = jnp.dot(hidden_part, down_part, preferred_element_type=jnp.float32)
        return running + lax.optimization_barrier(shard_sum.astype(jnp.bfloat16)).astype(jnp.float32)
    ffw_sum = lax.fori_loop(jnp.int32(0), jnp.int32(N_MP), ffw_shard, jnp.zeros((PROMPT_LEN_ALL, HIDDEN_BREADTH), jnp.float32))
    hidden_out = (after_attn.astype(jnp.float32) + rms_scale(ffw_sum, after_feedforward_gain)).astype(jnp.bfloat16)
    return (hidden_out, kv_new)
```

```python
import math

import jax
import jax.numpy as jnp
from jax import lax
from jax.sharding import PartitionSpec as P

HIDDEN_BREADTH = 4608
ASKING_CHANNELS = 32
CHANNEL_LENGTH = 128
NUM_LOW_TERMS = 64
LOW_DIMENSION = 16
SHARD_PROMPTS = 8
PPR = 4
PAGE = 16


EPS = 1e-06
SOFTCAP = 50.0

DP_AXES = ("zh", "c")
MP_AXES = ("x", "y", "zl")
MP_STAGES = (("zl",), ("x", "y"))


def gather_mp(values):
    for stage in MP_STAGES:
        values = lax.all_gather(values, stage, axis=0, tiled=True)
    return values


def scatter_mp(values):
    for stage in reversed(MP_STAGES):
        values = lax.psum_scatter(values, stage, scatter_dimension=0, tiled=True)
    return values


def sum_mp(values):
    for stage in MP_STAGES:
        values = lax.psum(values, stage)
    return values


def rms_scale(values, scaling):
    mean_square = jnp.mean(values * values, axis=-1, keepdims=True)
    return values * lax.rsqrt(mean_square + EPS) * scaling


def apply_rotary(values, token_positions):
    half_dim = values.shape[-1] // 2
    frequency = 10000.0 ** (-2.0 * jnp.arange(half_dim, dtype=jnp.float32) / values.shape[-1])
    angles = token_positions.astype(jnp.float32)[:, None] * frequency[None, :]
    cosine = jnp.cos(angles)[:, None, :]
    sine_part = jnp.sin(angles)[:, None, :]
    first_half = values[..., :half_dim]
    second_half = values[..., half_dim:]
    return jnp.concatenate(
        [
            first_half * cosine - second_half * sine_part,
            second_half * cosine + first_half * sine_part,
        ],
        axis=-1,
    )


def positions_of(segments):
    length = segments.shape[0]
    earlier = jnp.sum((segments[None, :] < segments[:, None]).astype(jnp.int32), axis=1)
    return PPR * PAGE + jnp.arange(length, dtype=jnp.int32) - earlier


def capped(scores):
    return SOFTCAP * jnp.tanh(scores / SOFTCAP)


def attend_local(query_rows, keys_new, fresh_values, keys_pre, values_pre, segments):
    scale_factor = 1.0 / math.sqrt(HIDDEN_BREADTH // ASKING_CHANNELS)
    length = segments.shape[0]
    prefix_owner = jnp.arange(keys_pre.shape[1], dtype=jnp.int32) // (PPR * PAGE)
    mask_pre = (prefix_owner[None, :] == segments[:, None])[None]
    ordinal = jnp.arange(length, dtype=jnp.int32)
    mask_new = ((segments[None, :] == segments[:, None]) & (ordinal[None, :] <= ordinal[:, None]))[
        None
    ]
    scores_pre = (
        jnp.einsum("thd,hjd->htj", query_rows, keys_pre, preferred_element_type=jnp.float32)
        * scale_factor
    )
    scores_new = (
        jnp.einsum("thd,uhd->htu", query_rows, keys_new, preferred_element_type=jnp.float32)
        * scale_factor
    )
    weight_pre = jnp.where(mask_pre, jnp.exp(capped(scores_pre)), 0.0)
    weight_new = jnp.where(mask_new, jnp.exp(capped(scores_new)), 0.0)
    totals = jnp.sum(weight_pre, axis=-1, keepdims=True) + jnp.sum(
        weight_new, axis=-1, keepdims=True
    )
    probs_pre = (weight_pre / totals).astype(jnp.bfloat16)
    probs_new = (weight_new / totals).astype(jnp.bfloat16)
    mixture = jnp.einsum("htj,hjd->thd", probs_pre, values_pre, preferred_element_type=jnp.float32)
    mixture = mixture + jnp.einsum(
        "htu,uhd->thd", probs_new, fresh_values, preferred_element_type=jnp.float32
    )
    return mixture.astype(jnp.bfloat16).reshape(length, -1)


def shards(
    residual_input,
    before_attention_gain,
    after_attention_gain,
    before_feedforward_gain,
    after_feedforward_gain,
    query_weight,
    key_value_weight,
    output_weight,
    gate_matrix,
    up_matrix,
    down_matrix,
    key_value_cache,
    projected_lowrank_left,
    projected_lowrank_right,
    result_lowrank_left,
    result_lowrank_right,
    token_request,
    lowrank_choice_by_prompt,
    adapter_position,
    request_pages,
):
    mp_index = lax.axis_index(MP_AXES)
    dp_index = lax.axis_index(DP_AXES)
    residual = residual_input.astype(jnp.float32)
    normed_rows = rms_scale(residual, before_attention_gain).astype(jnp.bfloat16)
    normalized_rows = gather_mp(normed_rows)
    prompt_ordinal = normalized_rows.shape[0]
    channel_window = query_weight.shape[1] // CHANNEL_LENGTH
    query_rows = jnp.dot(normalized_rows, query_weight, preferred_element_type=jnp.float32).reshape(
        prompt_ordinal, channel_window, CHANNEL_LENGTH
    )
    key_value_rows = jnp.dot(
        normalized_rows,
        key_value_weight.reshape(HIDDEN_BREADTH, 2 * channel_window * CHANNEL_LENGTH),
        preferred_element_type=jnp.float32,
    ).reshape(prompt_ordinal, 2, channel_window, CHANNEL_LENGTH)
    segments = token_request[0]
    request_ids = lowrank_choice_by_prompt[0]
    request_range = jnp.arange(SHARD_PROMPTS, dtype=jnp.int32)
    membership = segments[:, None] == request_range[None, :]
    adapter_range = jnp.arange(NUM_LOW_TERMS, dtype=jnp.int32)
    token_adapter = jnp.sum(jnp.where(membership, request_ids[None, :], 0), axis=1)
    token_adapter_slot = jnp.sum(
        jnp.where(token_adapter[:, None] == adapter_range[None, :], adapter_position[None, :], 0),
        axis=1,
    )
    seat_count = projected_lowrank_left.shape[0]
    local_seats = mp_index * seat_count + jnp.arange(seat_count, dtype=jnp.int32)
    seat_factors = jnp.einsum(
        "td,sdk->tsk", normalized_rows, projected_lowrank_left, preferred_element_type=jnp.float32
    )
    seat_here = token_adapter_slot[:, None] == local_seats[None, :]
    lowrank_source = jnp.sum(jnp.where(seat_here[:, :, None], seat_factors, 0.0), axis=1)
    lowrank_source = sum_mp(lowrank_source.astype(jnp.bfloat16))
    choice_mask_table = membership.astype(jnp.bfloat16)
    broadened_lines = (choice_mask_table[:, :, None] * lowrank_source[:, None, :]).reshape(
        prompt_ordinal, SHARD_PROMPTS * LOW_DIMENSION
    )
    raised_result_lines = projected_lowrank_right[request_ids].reshape(
        SHARD_PROMPTS * LOW_DIMENSION, 3 * channel_window * CHANNEL_LENGTH
    )
    adapter_query_key_value = jnp.dot(
        broadened_lines, raised_result_lines, preferred_element_type=jnp.float32
    ).reshape(prompt_ordinal, 3, channel_window, CHANNEL_LENGTH)
    token_positions = positions_of(segments)
    rotary_queries = apply_rotary(
        query_rows + adapter_query_key_value[:, 0], token_positions
    ).astype(jnp.bfloat16)
    rotary_keys = apply_rotary(
        key_value_rows[:, 0] + adapter_query_key_value[:, 1], token_positions
    ).astype(jnp.bfloat16)
    fresh_values = (key_value_rows[:, 1] + adapter_query_key_value[:, 2]).astype(jnp.bfloat16)
    kv_new = jnp.stack([rotary_keys, fresh_values], axis=1)
    own_pages = lax.dynamic_index_in_dim(request_pages, dp_index, 0, keepdims=False).reshape(
        SHARD_PROMPTS * PPR
    )
    whole_pool = lax.all_gather(key_value_cache, DP_AXES, axis=0, tiled=True)
    chosen = whole_pool[own_pages]
    keys_pre = jnp.transpose(chosen[:, 0], (1, 0, 2, 3)).reshape(
        channel_window, SHARD_PROMPTS * PPR * PAGE, CHANNEL_LENGTH
    )
    values_pre = jnp.transpose(chosen[:, 1], (1, 0, 2, 3)).reshape(
        channel_window, SHARD_PROMPTS * PPR * PAGE, CHANNEL_LENGTH
    )
    attended = attend_local(
        rotary_queries, rotary_keys, fresh_values, keys_pre, values_pre, segments
    )
    request_output_down = result_lowrank_left[request_ids]
    request_output_factors = jnp.einsum(
        "tc,rck->trk", attended, request_output_down, preferred_element_type=jnp.float32
    )
    output_adapter_piece = jnp.sum(
        jnp.where(membership[:, :, None], request_output_factors, 0.0), axis=1
    )
    result_lowrank_source = sum_mp(output_adapter_piece).astype(jnp.bfloat16)
    result_seat_lines = result_lowrank_right.shape[0]
    output_slots = mp_index * result_seat_lines + jnp.arange(result_seat_lines, dtype=jnp.int32)
    resident_here = (token_adapter_slot[:, None] == output_slots[None, :]).astype(jnp.bfloat16)
    broadened_result = (resident_here[:, :, None] * result_lowrank_source[:, None, :]).reshape(
        prompt_ordinal, result_seat_lines * LOW_DIMENSION
    )
    raised_window = result_lowrank_right.reshape(result_seat_lines * LOW_DIMENSION, HIDDEN_BREADTH)
    attn_sum = scatter_mp(
        (
            jnp.dot(attended, output_weight, preferred_element_type=jnp.float32)
            + jnp.dot(broadened_result, raised_window, preferred_element_type=jnp.float32)
        ).astype(jnp.bfloat16)
    ).astype(jnp.float32)
    after_attn = (residual + rms_scale(attn_sum, after_attention_gain)).astype(jnp.bfloat16)
    normed_ffw = rms_scale(after_attn.astype(jnp.float32), before_feedforward_gain).astype(
        jnp.bfloat16
    )
    piece = gather_mp(normed_ffw)
    gated = jnp.dot(piece, gate_matrix, preferred_element_type=jnp.float32)
    upward = jnp.dot(piece, up_matrix, preferred_element_type=jnp.float32)
    hidden = (jax.nn.gelu(gated, approximate=True) * upward).astype(jnp.bfloat16)
    ffw_sum = scatter_mp(
        jnp.dot(hidden, down_matrix, preferred_element_type=jnp.float32).astype(jnp.bfloat16)
    ).astype(jnp.float32)
    hidden_out = (
        after_attn.astype(jnp.float32) + rms_scale(ffw_sum, after_feedforward_gain)
    ).astype(jnp.bfloat16)
    return (hidden_out, kv_new)


def solution(mesh):
    fine_mesh = jax.sharding.Mesh(
        mesh.devices.reshape(2, 2, 4, 4, 2), DP_AXES + MP_AXES
    )
    return jax.shard_map(
        shards,
        mesh=fine_mesh,
        in_specs=(
            P(DP_AXES + MP_AXES, None),
            P(),
            P(),
            P(),
            P(),
            P(None, MP_AXES),
            P(None, None, MP_AXES, None),
            P(MP_AXES, None),
            P(None, MP_AXES),
            P(None, MP_AXES),
            P(MP_AXES, None),
            P(DP_AXES, None, MP_AXES, None, None),
            P(MP_AXES, None, None),
            P(None, None, None, MP_AXES, None),
            P(None, MP_AXES, None),
            P(MP_AXES, None, None),
            P(DP_AXES, None),
            P(DP_AXES, None),
            P(),
            P(),
        ),
        out_specs=(P(DP_AXES + MP_AXES, None), P(DP_AXES, None, MP_AXES, None)),
        check_vma=False,
    )
```

```python
import math

import jax
import jax.numpy as jnp
from jax import lax
from jax.sharding import PartitionSpec as P

HIDDEN_BREADTH = 4608
ASKING_CHANNELS = 32
CHANNEL_LENGTH = 128
NUM_LOW_TERMS = 64
LOW_DIMENSION = 16
SHARD_PROMPTS = 8
PPR = 4
PAGE = 16


EPS = 1e-06
SOFTCAP = 50.0

DP_AXES = ("zh", "c")
MP_AXES = ("x", "y", "zl")
MP_STAGES = (("zl",), ("x", "y"))


def gather_mp(values):
    for stage in MP_STAGES:
        values = lax.all_gather(values, stage, axis=0, tiled=True)
    return values


def scatter_mp(values):
    for stage in reversed(MP_STAGES):
        values = lax.psum_scatter(values, stage, scatter_dimension=0, tiled=True)
    return values


def sum_mp(values):
    for stage in (("zl",), ("y",), ("x",)):
        values = lax.psum(values, stage)
    return values


def rms_scale(values, scaling):
    mean_square = jnp.mean(values * values, axis=-1, keepdims=True)
    return values * lax.rsqrt(mean_square + EPS) * scaling


def apply_rotary(values, token_positions):
    half_dim = values.shape[-1] // 2
    frequency = 10000.0 ** (-2.0 * jnp.arange(half_dim, dtype=jnp.float32) / values.shape[-1])
    angles = token_positions.astype(jnp.float32)[:, None] * frequency[None, :]
    cosine = jnp.cos(angles)[:, None, :]
    sine_part = jnp.sin(angles)[:, None, :]
    first_half = values[..., :half_dim]
    second_half = values[..., half_dim:]
    return jnp.concatenate(
        [
            first_half * cosine - second_half * sine_part,
            second_half * cosine + first_half * sine_part,
        ],
        axis=-1,
    )


def positions_of(segments):
    length = segments.shape[0]
    earlier = jnp.sum((segments[None, :] < segments[:, None]).astype(jnp.int32), axis=1)
    return PPR * PAGE + jnp.arange(length, dtype=jnp.int32) - earlier


def capped(scores):
    return SOFTCAP * jnp.tanh(scores / SOFTCAP)


def attend_local(query_rows, keys_new, fresh_values, keys_pre, values_pre, segments):
    scale_factor = 1.0 / math.sqrt(HIDDEN_BREADTH // ASKING_CHANNELS)
    length = segments.shape[0]
    prefix_owner = jnp.arange(keys_pre.shape[1], dtype=jnp.int32) // (PPR * PAGE)
    mask_pre = (prefix_owner[None, :] == segments[:, None])[None]
    ordinal = jnp.arange(length, dtype=jnp.int32)
    mask_new = ((segments[None, :] == segments[:, None]) & (ordinal[None, :] <= ordinal[:, None]))[
        None
    ]
    scores_pre = (
        jnp.einsum("thd,hjd->htj", query_rows, keys_pre, preferred_element_type=jnp.float32)
        * scale_factor
    )
    scores_new = (
        jnp.einsum("thd,uhd->htu", query_rows, keys_new, preferred_element_type=jnp.float32)
        * scale_factor
    )
    weight_pre = jnp.where(mask_pre, jnp.exp(capped(scores_pre)), 0.0)
    weight_new = jnp.where(mask_new, jnp.exp(capped(scores_new)), 0.0)
    totals = jnp.sum(weight_pre, axis=-1, keepdims=True) + jnp.sum(
        weight_new, axis=-1, keepdims=True
    )
    probs_pre = (weight_pre / totals).astype(jnp.bfloat16)
    probs_new = (weight_new / totals).astype(jnp.bfloat16)
    mixture = jnp.einsum("htj,hjd->thd", probs_pre, values_pre, preferred_element_type=jnp.float32)
    mixture = mixture + jnp.einsum(
        "htu,uhd->thd", probs_new, fresh_values, preferred_element_type=jnp.float32
    )
    return mixture.astype(jnp.bfloat16).reshape(length, -1)


def shards(
    residual_input,
    before_attention_gain,
    after_attention_gain,
    before_feedforward_gain,
    after_feedforward_gain,
    query_weight,
    key_value_weight,
    output_weight,
    gate_matrix,
    up_matrix,
    down_matrix,
    key_value_cache,
    projected_lowrank_left,
    projected_lowrank_right,
    result_lowrank_left,
    result_lowrank_right,
    token_request,
    lowrank_choice_by_prompt,
    adapter_position,
    request_pages,
):
    mp_index = lax.axis_index(MP_AXES)
    dp_index = lax.axis_index(DP_AXES)
    residual = residual_input.astype(jnp.float32)
    normed_rows = rms_scale(residual, before_attention_gain).astype(jnp.bfloat16)
    normalized_rows = gather_mp(normed_rows)
    prompt_ordinal = normalized_rows.shape[0]
    channel_window = query_weight.shape[1] // CHANNEL_LENGTH
    query_rows = jnp.dot(normalized_rows, query_weight, preferred_element_type=jnp.float32).reshape(
        prompt_ordinal, channel_window, CHANNEL_LENGTH
    )
    key_value_rows = jnp.dot(
        normalized_rows,
        key_value_weight.reshape(HIDDEN_BREADTH, 2 * channel_window * CHANNEL_LENGTH),
        preferred_element_type=jnp.float32,
    ).reshape(prompt_ordinal, 2, channel_window, CHANNEL_LENGTH)
    segments = token_request[0]
    request_ids = lowrank_choice_by_prompt[0]
    request_range = jnp.arange(SHARD_PROMPTS, dtype=jnp.int32)
    membership = segments[:, None] == request_range[None, :]
    adapter_range = jnp.arange(NUM_LOW_TERMS, dtype=jnp.int32)
    token_adapter = jnp.sum(jnp.where(membership, request_ids[None, :], 0), axis=1)
    token_adapter_slot = jnp.sum(
        jnp.where(token_adapter[:, None] == adapter_range[None, :], adapter_position[None, :], 0),
        axis=1,
    )
    seat_count = projected_lowrank_left.shape[0]
    local_seats = mp_index * seat_count + jnp.arange(seat_count, dtype=jnp.int32)
    seat_factors = jnp.einsum(
        "td,sdk->tsk", normalized_rows, projected_lowrank_left, preferred_element_type=jnp.float32
    )
    seat_here = token_adapter_slot[:, None] == local_seats[None, :]
    lowrank_source = jnp.sum(jnp.where(seat_here[:, :, None], seat_factors, 0.0), axis=1)
    lowrank_source = sum_mp(lowrank_source).astype(jnp.bfloat16)
    choice_mask_table = membership.astype(jnp.bfloat16)
    broadened_lines = (choice_mask_table[:, :, None] * lowrank_source[:, None, :]).reshape(
        prompt_ordinal, SHARD_PROMPTS * LOW_DIMENSION
    )
    raised_result_lines = projected_lowrank_right[request_ids].reshape(
        SHARD_PROMPTS * LOW_DIMENSION, 3 * channel_window * CHANNEL_LENGTH
    )
    adapter_query_key_value = jnp.dot(
        broadened_lines, raised_result_lines, preferred_element_type=jnp.float32
    ).reshape(prompt_ordinal, 3, channel_window, CHANNEL_LENGTH)
    token_positions = positions_of(segments)
    rotary_queries = apply_rotary(
        query_rows + adapter_query_key_value[:, 0], token_positions
    ).astype(jnp.bfloat16)
    rotary_keys = apply_rotary(
        key_value_rows[:, 0] + adapter_query_key_value[:, 1], token_positions
    ).astype(jnp.bfloat16)
    fresh_values = (key_value_rows[:, 1] + adapter_query_key_value[:, 2]).astype(jnp.bfloat16)
    kv_new = jnp.stack([rotary_keys, fresh_values], axis=1)
    own_pages = lax.dynamic_index_in_dim(request_pages, dp_index, 0, keepdims=False).reshape(
        SHARD_PROMPTS * PPR
    )
    whole_pool = lax.all_gather(key_value_cache, DP_AXES, axis=0, tiled=True)
    chosen = whole_pool[own_pages]
    keys_pre = jnp.transpose(chosen[:, 0], (1, 0, 2, 3)).reshape(
        channel_window, SHARD_PROMPTS * PPR * PAGE, CHANNEL_LENGTH
    )
    values_pre = jnp.transpose(chosen[:, 1], (1, 0, 2, 3)).reshape(
        channel_window, SHARD_PROMPTS * PPR * PAGE, CHANNEL_LENGTH
    )
    attended = attend_local(
        rotary_queries, rotary_keys, fresh_values, keys_pre, values_pre, segments
    )
    request_output_down = result_lowrank_left[request_ids]
    request_output_factors = jnp.einsum(
        "tc,rck->trk", attended, request_output_down, preferred_element_type=jnp.float32
    )
    output_adapter_piece = jnp.sum(
        jnp.where(membership[:, :, None], request_output_factors, 0.0), axis=1
    )
    result_lowrank_source = sum_mp(output_adapter_piece).astype(jnp.bfloat16)
    result_seat_lines = result_lowrank_right.shape[0]
    output_slots = mp_index * result_seat_lines + jnp.arange(result_seat_lines, dtype=jnp.int32)
    resident_here = (token_adapter_slot[:, None] == output_slots[None, :]).astype(jnp.bfloat16)
    broadened_result = (resident_here[:, :, None] * result_lowrank_source[:, None, :]).reshape(
        prompt_ordinal, result_seat_lines * LOW_DIMENSION
    )
    raised_window = result_lowrank_right.reshape(result_seat_lines * LOW_DIMENSION, HIDDEN_BREADTH)
    attn_sum = scatter_mp(
        (
            jnp.dot(attended, output_weight, preferred_element_type=jnp.float32)
            + jnp.dot(broadened_result, raised_window, preferred_element_type=jnp.float32)
        ).astype(jnp.bfloat16)
    ).astype(jnp.float32)
    after_attn = (residual + rms_scale(attn_sum, after_attention_gain)).astype(jnp.bfloat16)
    normed_ffw = rms_scale(after_attn.astype(jnp.float32), before_feedforward_gain).astype(
        jnp.bfloat16
    )
    piece = gather_mp(normed_ffw)
    gated = jnp.dot(piece, gate_matrix, preferred_element_type=jnp.float32)
    upward = jnp.dot(piece, up_matrix, preferred_element_type=jnp.float32)
    hidden = (jax.nn.gelu(gated, approximate=True) * upward).astype(jnp.bfloat16)
    ffw_sum = scatter_mp(
        jnp.dot(hidden, down_matrix, preferred_element_type=jnp.float32).astype(jnp.bfloat16)
    ).astype(jnp.float32)
    hidden_out = (
        after_attn.astype(jnp.float32) + rms_scale(ffw_sum, after_feedforward_gain)
    ).astype(jnp.bfloat16)
    return (hidden_out, kv_new)


def solution(mesh):
    fine_mesh = jax.sharding.Mesh(
        mesh.devices.reshape(2, 2, 4, 4, 2), DP_AXES + MP_AXES
    )
    return jax.shard_map(
        shards,
        mesh=fine_mesh,
        in_specs=(
            P(DP_AXES + MP_AXES, None),
            P(),
            P(),
            P(),
            P(),
            P(None, MP_AXES),
            P(None, None, MP_AXES, None),
            P(MP_AXES, None),
            P(None, MP_AXES),
            P(None, MP_AXES),
            P(MP_AXES, None),
            P(DP_AXES, None, MP_AXES, None, None),
            P(MP_AXES, None, None),
            P(None, None, None, MP_AXES, None),
            P(None, MP_AXES, None),
            P(MP_AXES, None, None),
            P(DP_AXES, None),
            P(DP_AXES, None),
            P(),
            P(),
        ),
        out_specs=(P(DP_AXES + MP_AXES, None), P(DP_AXES, None, MP_AXES, None)),
        check_vma=False,
    )
```

```python
import math

import jax
import jax.numpy as jnp
from jax import lax
from jax.sharding import PartitionSpec as P

HIDDEN_BREADTH = 4608
ASKING_CHANNELS = 32
CHANNEL_LENGTH = 128
NUM_LOW_TERMS = 64
LOW_DIMENSION = 16
SHARD_PROMPTS = 8
PPR = 4
PAGE = 16


EPS = 1e-06
SOFTCAP = 50.0

DP_AXES = ("zh", "c")
MP_AXES = ("x", "y", "zl")


AXIS_SIZES = {"zh": 2, "c": 2, "x": 4, "y": 4, "zl": 2}
PAIR_SWAP = ((0, 1), (1, 0))


def gather_mp(values):
    other = lax.ppermute(values, "zl", perm=PAIR_SWAP)
    lead = lax.axis_index("zl") == 0
    values = jnp.concatenate(
        [jnp.where(lead, values, other), jnp.where(lead, other, values)], axis=0
    )
    return lax.all_gather(values, ("x", "y"), axis=0, tiled=True)


def scatter_mp(values):
    values = lax.psum_scatter(values, ("x", "y"), scatter_dimension=0, tiled=True)
    half = values.shape[0] // 2
    lead = lax.axis_index("zl") == 0
    keep = jnp.where(lead, values[:half], values[half:])
    send = jnp.where(lead, values[half:], values[:half])
    other = lax.ppermute(send, "zl", perm=PAIR_SWAP)
    return keep.astype(jnp.float32) + other.astype(jnp.float32)


def sum_mp(values):
    for name in ("zl", "y", "x"):
        step = 1
        while step < AXIS_SIZES[name]:
            partner = [(i, i ^ step) for i in range(AXIS_SIZES[name])]
            values = values + lax.ppermute(values, name, perm=partner)
            step *= 2
    return values


def rms_scale(values, scaling):
    mean_square = jnp.mean(values * values, axis=-1, keepdims=True)
    return values * lax.rsqrt(mean_square + EPS) * scaling


def apply_rotary(values, token_positions):
    half_dim = values.shape[-1] // 2
    frequency = 10000.0 ** (-2.0 * jnp.arange(half_dim, dtype=jnp.float32) / values.shape[-1])
    angles = token_positions.astype(jnp.float32)[:, None] * frequency[None, :]
    cosine = jnp.cos(angles)[:, None, :]
    sine_part = jnp.sin(angles)[:, None, :]
    first_half = values[..., :half_dim]
    second_half = values[..., half_dim:]
    return jnp.concatenate(
        [
            first_half * cosine - second_half * sine_part,
            second_half * cosine + first_half * sine_part,
        ],
        axis=-1,
    )


def positions_of(segments):
    length = segments.shape[0]
    earlier = jnp.sum((segments[None, :] < segments[:, None]).astype(jnp.int32), axis=1)
    return PPR * PAGE + jnp.arange(length, dtype=jnp.int32) - earlier


def capped(scores):
    return SOFTCAP * jnp.tanh(scores / SOFTCAP)


def attend_local(query_rows, keys_new, fresh_values, keys_pre, values_pre, segments):
    scale_factor = 1.0 / math.sqrt(HIDDEN_BREADTH // ASKING_CHANNELS)
    length = segments.shape[0]
    prefix_owner = jnp.arange(keys_pre.shape[1], dtype=jnp.int32) // (PPR * PAGE)
    mask_pre = (prefix_owner[None, :] == segments[:, None])[None]
    ordinal = jnp.arange(length, dtype=jnp.int32)
    mask_new = ((segments[None, :] == segments[:, None]) & (ordinal[None, :] <= ordinal[:, None]))[
        None
    ]
    scores_pre = (
        jnp.einsum("thd,hjd->htj", query_rows, keys_pre, preferred_element_type=jnp.float32)
        * scale_factor
    )
    scores_new = (
        jnp.einsum("thd,uhd->htu", query_rows, keys_new, preferred_element_type=jnp.float32)
        * scale_factor
    )
    weight_pre = jnp.where(mask_pre, jnp.exp(capped(scores_pre)), 0.0)
    weight_new = jnp.where(mask_new, jnp.exp(capped(scores_new)), 0.0)
    totals = jnp.sum(weight_pre, axis=-1, keepdims=True) + jnp.sum(
        weight_new, axis=-1, keepdims=True
    )
    probs_pre = (weight_pre / totals).astype(jnp.bfloat16)
    probs_new = (weight_new / totals).astype(jnp.bfloat16)
    mixture = jnp.einsum("htj,hjd->thd", probs_pre, values_pre, preferred_element_type=jnp.float32)
    mixture = mixture + jnp.einsum(
        "htu,uhd->thd", probs_new, fresh_values, preferred_element_type=jnp.float32
    )
    return mixture.astype(jnp.bfloat16).reshape(length, -1)


def shards(
    residual_input,
    before_attention_gain,
    after_attention_gain,
    before_feedforward_gain,
    after_feedforward_gain,
    query_weight,
    key_value_weight,
    output_weight,
    gate_matrix,
    up_matrix,
    down_matrix,
    key_value_cache,
    projected_lowrank_left,
    projected_lowrank_right,
    result_lowrank_left,
    result_lowrank_right,
    token_request,
    lowrank_choice_by_prompt,
    adapter_position,
    request_pages,
):
    mp_index = lax.axis_index(MP_AXES)
    dp_index = lax.axis_index(DP_AXES)
    residual = residual_input.astype(jnp.float32)
    normed_rows = rms_scale(residual, before_attention_gain).astype(jnp.bfloat16)
    normalized_rows = gather_mp(normed_rows)
    prompt_ordinal = normalized_rows.shape[0]
    channel_window = query_weight.shape[1] // CHANNEL_LENGTH
    query_rows = jnp.dot(normalized_rows, query_weight, preferred_element_type=jnp.float32).reshape(
        prompt_ordinal, channel_window, CHANNEL_LENGTH
    )
    key_value_rows = jnp.dot(
        normalized_rows,
        key_value_weight.reshape(HIDDEN_BREADTH, 2 * channel_window * CHANNEL_LENGTH),
        preferred_element_type=jnp.float32,
    ).reshape(prompt_ordinal, 2, channel_window, CHANNEL_LENGTH)
    segments = token_request[0]
    request_ids = lowrank_choice_by_prompt[0]
    request_range = jnp.arange(SHARD_PROMPTS, dtype=jnp.int32)
    membership = segments[:, None] == request_range[None, :]
    adapter_range = jnp.arange(NUM_LOW_TERMS, dtype=jnp.int32)
    token_adapter = jnp.sum(jnp.where(membership, request_ids[None, :], 0), axis=1)
    token_adapter_slot = jnp.sum(
        jnp.where(token_adapter[:, None] == adapter_range[None, :], adapter_position[None, :], 0),
        axis=1,
    )
    seat_count = projected_lowrank_left.shape[0]
    local_seats = mp_index * seat_count + jnp.arange(seat_count, dtype=jnp.int32)
    seat_factors = jnp.einsum(
        "td,sdk->tsk", normalized_rows, projected_lowrank_left, preferred_element_type=jnp.float32
    )
    seat_here = token_adapter_slot[:, None] == local_seats[None, :]
    lowrank_source = jnp.sum(jnp.where(seat_here[:, :, None], seat_factors, 0.0), axis=1)
    lowrank_source = sum_mp(lowrank_source).astype(jnp.bfloat16)
    choice_mask_table = membership.astype(jnp.bfloat16)
    broadened_lines = (choice_mask_table[:, :, None] * lowrank_source[:, None, :]).reshape(
        prompt_ordinal, SHARD_PROMPTS * LOW_DIMENSION
    )
    raised_result_lines = projected_lowrank_right[request_ids].reshape(
        SHARD_PROMPTS * LOW_DIMENSION, 3 * channel_window * CHANNEL_LENGTH
    )
    adapter_query_key_value = jnp.dot(
        broadened_lines, raised_result_lines, preferred_element_type=jnp.float32
    ).reshape(prompt_ordinal, 3, channel_window, CHANNEL_LENGTH)
    token_positions = positions_of(segments)
    rotary_queries = apply_rotary(
        query_rows + adapter_query_key_value[:, 0], token_positions
    ).astype(jnp.bfloat16)
    rotary_keys = apply_rotary(
        key_value_rows[:, 0] + adapter_query_key_value[:, 1], token_positions
    ).astype(jnp.bfloat16)
    fresh_values = (key_value_rows[:, 1] + adapter_query_key_value[:, 2]).astype(jnp.bfloat16)
    kv_new = jnp.stack([rotary_keys, fresh_values], axis=1)
    own_pages = lax.dynamic_index_in_dim(request_pages, dp_index, 0, keepdims=False).reshape(
        SHARD_PROMPTS * PPR
    )
    whole_pool = lax.all_gather(key_value_cache, DP_AXES, axis=0, tiled=True)
    chosen = whole_pool[own_pages]
    keys_pre = jnp.transpose(chosen[:, 0], (1, 0, 2, 3)).reshape(
        channel_window, SHARD_PROMPTS * PPR * PAGE, CHANNEL_LENGTH
    )
    values_pre = jnp.transpose(chosen[:, 1], (1, 0, 2, 3)).reshape(
        channel_window, SHARD_PROMPTS * PPR * PAGE, CHANNEL_LENGTH
    )
    attended = attend_local(
        rotary_queries, rotary_keys, fresh_values, keys_pre, values_pre, segments
    )
    request_output_down = result_lowrank_left[request_ids]
    request_output_factors = jnp.einsum(
        "tc,rck->trk", attended, request_output_down, preferred_element_type=jnp.float32
    )
    output_adapter_piece = jnp.sum(
        jnp.where(membership[:, :, None], request_output_factors, 0.0), axis=1
    )
    result_lowrank_source = sum_mp(output_adapter_piece).astype(jnp.bfloat16)
    result_seat_lines = result_lowrank_right.shape[0]
    output_slots = mp_index * result_seat_lines + jnp.arange(result_seat_lines, dtype=jnp.int32)
    resident_here = (token_adapter_slot[:, None] == output_slots[None, :]).astype(jnp.bfloat16)
    broadened_result = (resident_here[:, :, None] * result_lowrank_source[:, None, :]).reshape(
        prompt_ordinal, result_seat_lines * LOW_DIMENSION
    )
    raised_window = result_lowrank_right.reshape(result_seat_lines * LOW_DIMENSION, HIDDEN_BREADTH)
    attn_sum = scatter_mp(
        (
            jnp.dot(attended, output_weight, preferred_element_type=jnp.float32)
            + jnp.dot(broadened_result, raised_window, preferred_element_type=jnp.float32)
        ).astype(jnp.bfloat16)
    ).astype(jnp.float32)
    after_attn = (residual + rms_scale(attn_sum, after_attention_gain)).astype(jnp.bfloat16)
    normed_ffw = rms_scale(after_attn.astype(jnp.float32), before_feedforward_gain).astype(
        jnp.bfloat16
    )
    piece = gather_mp(normed_ffw)
    gated = jnp.dot(piece, gate_matrix, preferred_element_type=jnp.float32)
    upward = jnp.dot(piece, up_matrix, preferred_element_type=jnp.float32)
    hidden = (jax.nn.gelu(gated, approximate=True) * upward).astype(jnp.bfloat16)
    ffw_sum = scatter_mp(
        jnp.dot(hidden, down_matrix, preferred_element_type=jnp.float32).astype(jnp.bfloat16)
    ).astype(jnp.float32)
    hidden_out = (
        after_attn.astype(jnp.float32) + rms_scale(ffw_sum, after_feedforward_gain)
    ).astype(jnp.bfloat16)
    return (hidden_out, kv_new)


def solution(mesh):
    fine_mesh = jax.sharding.Mesh(
        mesh.devices.reshape(2, 2, 4, 4, 2), DP_AXES + MP_AXES
    )
    return jax.shard_map(
        shards,
        mesh=fine_mesh,
        in_specs=(
            P(DP_AXES + MP_AXES, None),
            P(),
            P(),
            P(),
            P(),
            P(None, MP_AXES),
            P(None, None, MP_AXES, None),
            P(MP_AXES, None),
            P(None, MP_AXES),
            P(None, MP_AXES),
            P(MP_AXES, None),
            P(DP_AXES, None, MP_AXES, None, None),
            P(MP_AXES, None, None),
            P(None, None, None, MP_AXES, None),
            P(None, MP_AXES, None),
            P(MP_AXES, None, None),
            P(DP_AXES, None),
            P(DP_AXES, None),
            P(),
            P(),
        ),
        out_specs=(P(DP_AXES + MP_AXES, None), P(DP_AXES, None, MP_AXES, None)),
        check_vma=False,
    )
```

```python
import math

import jax
import jax.numpy as jnp
from jax import lax
from jax.sharding import PartitionSpec as P

HIDDEN_BREADTH = 4608
ASKING_CHANNELS = 32
CHANNEL_LENGTH = 128
NUM_LOW_TERMS = 64
LOW_DIMENSION = 16
SHARD_PROMPTS = 8
PPR = 4
PAGE = 16


EPS = 1e-06
SOFTCAP = 50.0

DP_AXES = ("zh", "c")
MP_AXES = ("x", "y", "zl")


AXIS_SIZES = {"zh": 2, "c": 2, "x": 4, "y": 4, "zl": 2}
PAIR_SWAP = ((0, 1), (1, 0))


PLANE_FLOWS = (("x", 1), ("x", -1), ("y", 1), ("y", -1))


def ring_gather(block, name, direction):
    size = AXIS_SIZES[name]
    me = lax.axis_index(name)
    perm = [(i, (i + direction) % size) for i in range(size)]
    gathered = jnp.zeros((size,) + block.shape, block.dtype)
    gathered = lax.dynamic_update_index_in_dim(gathered, block, me, 0)
    moving = block
    for step in range(size - 1):
        moving = lax.ppermute(moving, name, perm=perm)
        source = jnp.remainder(me - direction * (step + 1), size)
        gathered = lax.dynamic_update_index_in_dim(gathered, moving, source, 0)
    return gathered


def ring_scatter(blocks, name, direction):
    size = AXIS_SIZES[name]
    me = lax.axis_index(name)
    perm = [(i, (i + direction) % size) for i in range(size)]

    def own(offset):
        index = jnp.remainder(me + offset, size)
        return lax.dynamic_index_in_dim(blocks, index, 0, keepdims=False).astype(jnp.float32)

    moving = own(-direction).astype(blocks.dtype)
    for step in range(size - 1):
        arrived = lax.ppermute(moving, name, perm=perm).astype(jnp.float32)
        if step < size - 2:
            moving = (arrived + own(-direction * (step + 2))).astype(blocks.dtype)
    return arrived + own(0)


def gather_plane(values):
    quarter = values.shape[-1] // len(PLANE_FLOWS)
    pieces = []
    for index, (first, direction) in enumerate(PLANE_FLOWS):
        part = values[:, index * quarter:(index + 1) * quarter]
        if first == "x":
            part = ring_gather(ring_gather(part, "y", direction), "x", direction)
        else:
            part = jnp.swapaxes(ring_gather(ring_gather(part, "x", direction), "y", direction), 0, 1)
        pieces.append(part.reshape(-1, quarter))
    return jnp.concatenate(pieces, axis=-1)


def scatter_plane(values):
    quarter = values.shape[-1] // len(PLANE_FLOWS)
    rows = values.reshape(AXIS_SIZES["x"], AXIS_SIZES["y"], -1, values.shape[-1])
    pieces = []
    for index, (first, direction) in enumerate(PLANE_FLOWS):
        part = rows[..., index * quarter:(index + 1) * quarter]
        if first == "x":
            part = ring_scatter(part, "x", direction).astype(values.dtype)
            part = ring_scatter(part, "y", direction)
        else:
            part = ring_scatter(jnp.swapaxes(part, 0, 1), "y", direction).astype(values.dtype)
            part = ring_scatter(part, "x", direction)
        pieces.append(part)
    return jnp.concatenate(pieces, axis=-1)


def gather_mp(values):
    other = lax.ppermute(values, "zl", perm=PAIR_SWAP)
    lead = lax.axis_index("zl") == 0
    values = jnp.concatenate(
        [jnp.where(lead, values, other), jnp.where(lead, other, values)], axis=0
    )
    return gather_plane(values)


def scatter_mp(values):
    values = scatter_plane(values)
    half = values.shape[0] // 2
    lead = lax.axis_index("zl") == 0
    keep = jnp.where(lead, values[:half], values[half:])
    send = jnp.where(lead, values[half:], values[:half]).astype(jnp.bfloat16)
    other = lax.ppermute(send, "zl", perm=PAIR_SWAP)
    return keep + other.astype(jnp.float32)


def sum_mp(values):
    for name in ("zl", "y", "x"):
        step = 1
        while step < AXIS_SIZES[name]:
            partner = [(i, i ^ step) for i in range(AXIS_SIZES[name])]
            values = values + lax.ppermute(values, name, perm=partner)
            step *= 2
    return values


def rms_scale(values, scaling):
    mean_square = jnp.mean(values * values, axis=-1, keepdims=True)
    return values * lax.rsqrt(mean_square + EPS) * scaling


def apply_rotary(values, token_positions):
    half_dim = values.shape[-1] // 2
    frequency = 10000.0 ** (-2.0 * jnp.arange(half_dim, dtype=jnp.float32) / values.shape[-1])
    angles = token_positions.astype(jnp.float32)[:, None] * frequency[None, :]
    cosine = jnp.cos(angles)[:, None, :]
    sine_part = jnp.sin(angles)[:, None, :]
    first_half = values[..., :half_dim]
    second_half = values[..., half_dim:]
    return jnp.concatenate(
        [
            first_half * cosine - second_half * sine_part,
            second_half * cosine + first_half * sine_part,
        ],
        axis=-1,
    )


def positions_of(segments):
    length = segments.shape[0]
    earlier = jnp.sum((segments[None, :] < segments[:, None]).astype(jnp.int32), axis=1)
    return PPR * PAGE + jnp.arange(length, dtype=jnp.int32) - earlier


def capped(scores):
    return SOFTCAP * jnp.tanh(scores / SOFTCAP)


def attend_local(query_rows, keys_new, fresh_values, keys_pre, values_pre, segments):
    scale_factor = 1.0 / math.sqrt(HIDDEN_BREADTH // ASKING_CHANNELS)
    length = segments.shape[0]
    prefix_owner = jnp.arange(keys_pre.shape[1], dtype=jnp.int32) // (PPR * PAGE)
    mask_pre = (prefix_owner[None, :] == segments[:, None])[None]
    ordinal = jnp.arange(length, dtype=jnp.int32)
    mask_new = ((segments[None, :] == segments[:, None]) & (ordinal[None, :] <= ordinal[:, None]))[
        None
    ]
    scores_pre = (
        jnp.einsum("thd,hjd->htj", query_rows, keys_pre, preferred_element_type=jnp.float32)
        * scale_factor
    )
    scores_new = (
        jnp.einsum("thd,uhd->htu", query_rows, keys_new, preferred_element_type=jnp.float32)
        * scale_factor
    )
    weight_pre = jnp.where(mask_pre, jnp.exp(capped(scores_pre)), 0.0)
    weight_new = jnp.where(mask_new, jnp.exp(capped(scores_new)), 0.0)
    totals = jnp.sum(weight_pre, axis=-1, keepdims=True) + jnp.sum(
        weight_new, axis=-1, keepdims=True
    )
    probs_pre = (weight_pre / totals).astype(jnp.bfloat16)
    probs_new = (weight_new / totals).astype(jnp.bfloat16)
    mixture = jnp.einsum("htj,hjd->thd", probs_pre, values_pre, preferred_element_type=jnp.float32)
    mixture = mixture + jnp.einsum(
        "htu,uhd->thd", probs_new, fresh_values, preferred_element_type=jnp.float32
    )
    return mixture.astype(jnp.bfloat16).reshape(length, -1)


def shards(
    residual_input,
    before_attention_gain,
    after_attention_gain,
    before_feedforward_gain,
    after_feedforward_gain,
    query_weight,
    key_value_weight,
    output_weight,
    gate_matrix,
    up_matrix,
    down_matrix,
    key_value_cache,
    projected_lowrank_left,
    projected_lowrank_right,
    result_lowrank_left,
    result_lowrank_right,
    token_request,
    lowrank_choice_by_prompt,
    adapter_position,
    request_pages,
):
    mp_index = lax.axis_index(MP_AXES)
    dp_index = lax.axis_index(DP_AXES)
    residual = residual_input.astype(jnp.float32)
    normed_rows = rms_scale(residual, before_attention_gain).astype(jnp.bfloat16)
    normalized_rows = gather_mp(normed_rows)
    prompt_ordinal = normalized_rows.shape[0]
    channel_window = query_weight.shape[1] // CHANNEL_LENGTH
    query_rows = jnp.dot(normalized_rows, query_weight, preferred_element_type=jnp.float32).reshape(
        prompt_ordinal, channel_window, CHANNEL_LENGTH
    )
    key_value_rows = jnp.dot(
        normalized_rows,
        key_value_weight.reshape(HIDDEN_BREADTH, 2 * channel_window * CHANNEL_LENGTH),
        preferred_element_type=jnp.float32,
    ).reshape(prompt_ordinal, 2, channel_window, CHANNEL_LENGTH)
    segments = token_request[0]
    request_ids = lowrank_choice_by_prompt[0]
    request_range = jnp.arange(SHARD_PROMPTS, dtype=jnp.int32)
    membership = segments[:, None] == request_range[None, :]
    adapter_range = jnp.arange(NUM_LOW_TERMS, dtype=jnp.int32)
    token_adapter = jnp.sum(jnp.where(membership, request_ids[None, :], 0), axis=1)
    token_adapter_slot = jnp.sum(
        jnp.where(token_adapter[:, None] == adapter_range[None, :], adapter_position[None, :], 0),
        axis=1,
    )
    seat_count = projected_lowrank_left.shape[0]
    local_seats = mp_index * seat_count + jnp.arange(seat_count, dtype=jnp.int32)
    seat_factors = jnp.einsum(
        "td,sdk->tsk", normalized_rows, projected_lowrank_left, preferred_element_type=jnp.float32
    )
    seat_here = token_adapter_slot[:, None] == local_seats[None, :]
    lowrank_source = jnp.sum(jnp.where(seat_here[:, :, None], seat_factors, 0.0), axis=1)
    lowrank_source = sum_mp(lowrank_source).astype(jnp.bfloat16)
    choice_mask_table = membership.astype(jnp.bfloat16)
    broadened_lines = (choice_mask_table[:, :, None] * lowrank_source[:, None, :]).reshape(
        prompt_ordinal, SHARD_PROMPTS * LOW_DIMENSION
    )
    raised_result_lines = projected_lowrank_right[request_ids].reshape(
        SHARD_PROMPTS * LOW_DIMENSION, 3 * channel_window * CHANNEL_LENGTH
    )
    adapter_query_key_value = jnp.dot(
        broadened_lines, raised_result_lines, preferred_element_type=jnp.float32
    ).reshape(prompt_ordinal, 3, channel_window, CHANNEL_LENGTH)
    token_positions = positions_of(segments)
    rotary_queries = apply_rotary(
        query_rows + adapter_query_key_value[:, 0], token_positions
    ).astype(jnp.bfloat16)
    rotary_keys = apply_rotary(
        key_value_rows[:, 0] + adapter_query_key_value[:, 1], token_positions
    ).astype(jnp.bfloat16)
    fresh_values = (key_value_rows[:, 1] + adapter_query_key_value[:, 2]).astype(jnp.bfloat16)
    kv_new = jnp.stack([rotary_keys, fresh_values], axis=1)
    own_pages = lax.dynamic_index_in_dim(request_pages, dp_index, 0, keepdims=False).reshape(
        SHARD_PROMPTS * PPR
    )
    whole_pool = lax.all_gather(key_value_cache, DP_AXES, axis=0, tiled=True)
    chosen = whole_pool[own_pages]
    keys_pre = jnp.transpose(chosen[:, 0], (1, 0, 2, 3)).reshape(
        channel_window, SHARD_PROMPTS * PPR * PAGE, CHANNEL_LENGTH
    )
    values_pre = jnp.transpose(chosen[:, 1], (1, 0, 2, 3)).reshape(
        channel_window, SHARD_PROMPTS * PPR * PAGE, CHANNEL_LENGTH
    )
    attended = attend_local(
        rotary_queries, rotary_keys, fresh_values, keys_pre, values_pre, segments
    )
    request_output_down = result_lowrank_left[request_ids]
    request_output_factors = jnp.einsum(
        "tc,rck->trk", attended, request_output_down, preferred_element_type=jnp.float32
    )
    output_adapter_piece = jnp.sum(
        jnp.where(membership[:, :, None], request_output_factors, 0.0), axis=1
    )
    result_lowrank_source = sum_mp(output_adapter_piece).astype(jnp.bfloat16)
    result_seat_lines = result_lowrank_right.shape[0]
    output_slots = mp_index * result_seat_lines + jnp.arange(result_seat_lines, dtype=jnp.int32)
    resident_here = (token_adapter_slot[:, None] == output_slots[None, :]).astype(jnp.bfloat16)
    broadened_result = (resident_here[:, :, None] * result_lowrank_source[:, None, :]).reshape(
        prompt_ordinal, result_seat_lines * LOW_DIMENSION
    )
    raised_window = result_lowrank_right.reshape(result_seat_lines * LOW_DIMENSION, HIDDEN_BREADTH)
    attn_sum = scatter_mp(
        (
            jnp.dot(attended, output_weight, preferred_element_type=jnp.float32)
            + jnp.dot(broadened_result, raised_window, preferred_element_type=jnp.float32)
        ).astype(jnp.bfloat16)
    ).astype(jnp.float32)
    after_attn = (residual + rms_scale(attn_sum, after_attention_gain)).astype(jnp.bfloat16)
    normed_ffw = rms_scale(after_attn.astype(jnp.float32), before_feedforward_gain).astype(
        jnp.bfloat16
    )
    piece = gather_mp(normed_ffw)
    gated = jnp.dot(piece, gate_matrix, preferred_element_type=jnp.float32)
    upward = jnp.dot(piece, up_matrix, preferred_element_type=jnp.float32)
    hidden = (jax.nn.gelu(gated, approximate=True) * upward).astype(jnp.bfloat16)
    ffw_sum = scatter_mp(
        jnp.dot(hidden, down_matrix, preferred_element_type=jnp.float32).astype(jnp.bfloat16)
    ).astype(jnp.float32)
    hidden_out = (
        after_attn.astype(jnp.float32) + rms_scale(ffw_sum, after_feedforward_gain)
    ).astype(jnp.bfloat16)
    return (hidden_out, kv_new)


def solution(mesh):
    fine_mesh = jax.sharding.Mesh(
        mesh.devices.reshape(2, 2, 4, 4, 2), DP_AXES + MP_AXES
    )
    return jax.shard_map(
        shards,
        mesh=fine_mesh,
        in_specs=(
            P(DP_AXES + MP_AXES, None),
            P(),
            P(),
            P(),
            P(),
            P(None, MP_AXES),
            P(None, None, MP_AXES, None),
            P(MP_AXES, None),
            P(None, MP_AXES),
            P(None, MP_AXES),
            P(MP_AXES, None),
            P(DP_AXES, None, MP_AXES, None, None),
            P(MP_AXES, None, None),
            P(None, None, None, MP_AXES, None),
            P(None, MP_AXES, None),
            P(MP_AXES, None, None),
            P(DP_AXES, None),
            P(DP_AXES, None),
            P(),
            P(),
        ),
        out_specs=(P(DP_AXES + MP_AXES, None), P(DP_AXES, None, MP_AXES, None)),
        check_vma=False,
    )
```

```python
import math

import jax
import jax.numpy as jnp
from jax import lax
from jax.sharding import PartitionSpec as P

HIDDEN_BREADTH = 4608
ASKING_CHANNELS = 32
CHANNEL_LENGTH = 128
NUM_LOW_TERMS = 64
LOW_DIMENSION = 16
SHARD_PROMPTS = 8
PPR = 4
PAGE = 16


EPS = 1e-06
SOFTCAP = 50.0

DP_AXES = ("zh", "c")
MP_AXES = ("x", "y", "zl")


AXIS_SIZES = {"zh": 2, "c": 2, "x": 4, "y": 4, "zl": 2}
PAIR_SWAP = ((0, 1), (1, 0))


PLANE_FLOWS = (("x", 1), ("y", -1))


def ring_gather(block, name, direction):
    size = AXIS_SIZES[name]
    me = lax.axis_index(name)
    perm = [(i, (i + direction) % size) for i in range(size)]
    gathered = jnp.zeros((size,) + block.shape, block.dtype)
    gathered = lax.dynamic_update_index_in_dim(gathered, block, me, 0)
    moving = block
    for step in range(size - 1):
        moving = lax.ppermute(moving, name, perm=perm)
        source = jnp.remainder(me - direction * (step + 1), size)
        gathered = lax.dynamic_update_index_in_dim(gathered, moving, source, 0)
    return gathered


def ring_scatter(blocks, name, direction):
    size = AXIS_SIZES[name]
    me = lax.axis_index(name)
    perm = [(i, (i + direction) % size) for i in range(size)]

    def own(offset):
        index = jnp.remainder(me + offset, size)
        return lax.dynamic_index_in_dim(blocks, index, 0, keepdims=False).astype(jnp.float32)

    moving = own(-direction).astype(blocks.dtype)
    for step in range(size - 1):
        arrived = lax.ppermute(moving, name, perm=perm).astype(jnp.float32)
        if step < size - 2:
            moving = (arrived + own(-direction * (step + 2))).astype(blocks.dtype)
    return arrived + own(0)


def gather_plane(values):
    quarter = values.shape[-1] // len(PLANE_FLOWS)
    pieces = []
    for index, (first, direction) in enumerate(PLANE_FLOWS):
        part = values[:, index * quarter:(index + 1) * quarter]
        if first == "x":
            part = ring_gather(ring_gather(part, "y", direction), "x", direction)
        else:
            part = jnp.swapaxes(ring_gather(ring_gather(part, "x", direction), "y", direction), 0, 1)
        pieces.append(part.reshape(-1, quarter))
    return jnp.concatenate(pieces, axis=-1)


def scatter_plane(values):
    quarter = values.shape[-1] // len(PLANE_FLOWS)
    rows = values.reshape(AXIS_SIZES["x"], AXIS_SIZES["y"], -1, values.shape[-1])
    pieces = []
    for index, (first, direction) in enumerate(PLANE_FLOWS):
        part = rows[..., index * quarter:(index + 1) * quarter]
        if first == "x":
            part = ring_scatter(part, "x", direction).astype(values.dtype)
            part = ring_scatter(part, "y", direction)
        else:
            part = ring_scatter(jnp.swapaxes(part, 0, 1), "y", direction).astype(values.dtype)
            part = ring_scatter(part, "x", direction)
        pieces.append(part)
    return jnp.concatenate(pieces, axis=-1)


def gather_mp(values):
    other = lax.ppermute(values, "zl", perm=PAIR_SWAP)
    lead = lax.axis_index("zl") == 0
    values = jnp.concatenate(
        [jnp.where(lead, values, other), jnp.where(lead, other, values)], axis=0
    )
    return gather_plane(values)


def scatter_mp(values):
    values = scatter_plane(values)
    half = values.shape[0] // 2
    lead = lax.axis_index("zl") == 0
    keep = jnp.where(lead, values[:half], values[half:])
    send = jnp.where(lead, values[half:], values[:half]).astype(jnp.bfloat16)
    other = lax.ppermute(send, "zl", perm=PAIR_SWAP)
    return keep + other.astype(jnp.float32)


def sum_mp(values):
    for name in ("zl", "y", "x"):
        step = 1
        while step < AXIS_SIZES[name]:
            partner = [(i, i ^ step) for i in range(AXIS_SIZES[name])]
            values = values + lax.ppermute(values, name, perm=partner)
            step *= 2
    return values


def rms_scale(values, scaling):
    mean_square = jnp.mean(values * values, axis=-1, keepdims=True)
    return values * lax.rsqrt(mean_square + EPS) * scaling


def apply_rotary(values, token_positions):
    half_dim = values.shape[-1] // 2
    frequency = 10000.0 ** (-2.0 * jnp.arange(half_dim, dtype=jnp.float32) / values.shape[-1])
    angles = token_positions.astype(jnp.float32)[:, None] * frequency[None, :]
    cosine = jnp.cos(angles)[:, None, :]
    sine_part = jnp.sin(angles)[:, None, :]
    first_half = values[..., :half_dim]
    second_half = values[..., half_dim:]
    return jnp.concatenate(
        [
            first_half * cosine - second_half * sine_part,
            second_half * cosine + first_half * sine_part,
        ],
        axis=-1,
    )


def positions_of(segments):
    length = segments.shape[0]
    earlier = jnp.sum((segments[None, :] < segments[:, None]).astype(jnp.int32), axis=1)
    return PPR * PAGE + jnp.arange(length, dtype=jnp.int32) - earlier


def capped(scores):
    return SOFTCAP * jnp.tanh(scores / SOFTCAP)


def attend_local(query_rows, keys_new, fresh_values, keys_pre, values_pre, segments):
    scale_factor = 1.0 / math.sqrt(HIDDEN_BREADTH // ASKING_CHANNELS)
    length = segments.shape[0]
    prefix_owner = jnp.arange(keys_pre.shape[1], dtype=jnp.int32) // (PPR * PAGE)
    mask_pre = (prefix_owner[None, :] == segments[:, None])[None]
    ordinal = jnp.arange(length, dtype=jnp.int32)
    mask_new = ((segments[None, :] == segments[:, None]) & (ordinal[None, :] <= ordinal[:, None]))[
        None
    ]
    scores_pre = (
        jnp.einsum("thd,hjd->htj", query_rows, keys_pre, preferred_element_type=jnp.float32)
        * scale_factor
    )
    scores_new = (
        jnp.einsum("thd,uhd->htu", query_rows, keys_new, preferred_element_type=jnp.float32)
        * scale_factor
    )
    weight_pre = jnp.where(mask_pre, jnp.exp(capped(scores_pre)), 0.0)
    weight_new = jnp.where(mask_new, jnp.exp(capped(scores_new)), 0.0)
    totals = jnp.sum(weight_pre, axis=-1, keepdims=True) + jnp.sum(
        weight_new, axis=-1, keepdims=True
    )
    probs_pre = (weight_pre / totals).astype(jnp.bfloat16)
    probs_new = (weight_new / totals).astype(jnp.bfloat16)
    mixture = jnp.einsum("htj,hjd->thd", probs_pre, values_pre, preferred_element_type=jnp.float32)
    mixture = mixture + jnp.einsum(
        "htu,uhd->thd", probs_new, fresh_values, preferred_element_type=jnp.float32
    )
    return mixture.astype(jnp.bfloat16).reshape(length, -1)


def shards(
    residual_input,
    before_attention_gain,
    after_attention_gain,
    before_feedforward_gain,
    after_feedforward_gain,
    query_weight,
    key_value_weight,
    output_weight,
    gate_matrix,
    up_matrix,
    down_matrix,
    key_value_cache,
    projected_lowrank_left,
    projected_lowrank_right,
    result_lowrank_left,
    result_lowrank_right,
    token_request,
    lowrank_choice_by_prompt,
    adapter_position,
    request_pages,
):
    mp_index = lax.axis_index(MP_AXES)
    dp_index = lax.axis_index(DP_AXES)
    residual = residual_input.astype(jnp.float32)
    normed_rows = rms_scale(residual, before_attention_gain).astype(jnp.bfloat16)
    normalized_rows = gather_mp(normed_rows)
    prompt_ordinal = normalized_rows.shape[0]
    channel_window = query_weight.shape[1] // CHANNEL_LENGTH
    query_rows = jnp.dot(normalized_rows, query_weight, preferred_element_type=jnp.float32).reshape(
        prompt_ordinal, channel_window, CHANNEL_LENGTH
    )
    key_value_rows = jnp.dot(
        normalized_rows,
        key_value_weight.reshape(HIDDEN_BREADTH, 2 * channel_window * CHANNEL_LENGTH),
        preferred_element_type=jnp.float32,
    ).reshape(prompt_ordinal, 2, channel_window, CHANNEL_LENGTH)
    segments = token_request[0]
    request_ids = lowrank_choice_by_prompt[0]
    request_range = jnp.arange(SHARD_PROMPTS, dtype=jnp.int32)
    membership = segments[:, None] == request_range[None, :]
    adapter_range = jnp.arange(NUM_LOW_TERMS, dtype=jnp.int32)
    token_adapter = jnp.sum(jnp.where(membership, request_ids[None, :], 0), axis=1)
    token_adapter_slot = jnp.sum(
        jnp.where(token_adapter[:, None] == adapter_range[None, :], adapter_position[None, :], 0),
        axis=1,
    )
    seat_count = projected_lowrank_left.shape[0]
    local_seats = mp_index * seat_count + jnp.arange(seat_count, dtype=jnp.int32)
    seat_factors = jnp.einsum(
        "td,sdk->tsk", normalized_rows, projected_lowrank_left, preferred_element_type=jnp.float32
    )
    seat_here = token_adapter_slot[:, None] == local_seats[None, :]
    lowrank_source = jnp.sum(jnp.where(seat_here[:, :, None], seat_factors, 0.0), axis=1)
    lowrank_source = sum_mp(lowrank_source).astype(jnp.bfloat16)
    choice_mask_table = membership.astype(jnp.bfloat16)
    broadened_lines = (choice_mask_table[:, :, None] * lowrank_source[:, None, :]).reshape(
        prompt_ordinal, SHARD_PROMPTS * LOW_DIMENSION
    )
    raised_result_lines = projected_lowrank_right[request_ids].reshape(
        SHARD_PROMPTS * LOW_DIMENSION, 3 * channel_window * CHANNEL_LENGTH
    )
    adapter_query_key_value = jnp.dot(
        broadened_lines, raised_result_lines, preferred_element_type=jnp.float32
    ).reshape(prompt_ordinal, 3, channel_window, CHANNEL_LENGTH)
    token_positions = positions_of(segments)
    rotary_queries = apply_rotary(
        query_rows + adapter_query_key_value[:, 0], token_positions
    ).astype(jnp.bfloat16)
    rotary_keys = apply_rotary(
        key_value_rows[:, 0] + adapter_query_key_value[:, 1], token_positions
    ).astype(jnp.bfloat16)
    fresh_values = (key_value_rows[:, 1] + adapter_query_key_value[:, 2]).astype(jnp.bfloat16)
    kv_new = jnp.stack([rotary_keys, fresh_values], axis=1)
    own_pages = lax.dynamic_index_in_dim(request_pages, dp_index, 0, keepdims=False).reshape(
        SHARD_PROMPTS * PPR
    )
    whole_pool = lax.all_gather(key_value_cache, DP_AXES, axis=0, tiled=True)
    chosen = whole_pool[own_pages]
    keys_pre = jnp.transpose(chosen[:, 0], (1, 0, 2, 3)).reshape(
        channel_window, SHARD_PROMPTS * PPR * PAGE, CHANNEL_LENGTH
    )
    values_pre = jnp.transpose(chosen[:, 1], (1, 0, 2, 3)).reshape(
        channel_window, SHARD_PROMPTS * PPR * PAGE, CHANNEL_LENGTH
    )
    attended = attend_local(
        rotary_queries, rotary_keys, fresh_values, keys_pre, values_pre, segments
    )
    request_output_down = result_lowrank_left[request_ids]
    request_output_factors = jnp.einsum(
        "tc,rck->trk", attended, request_output_down, preferred_element_type=jnp.float32
    )
    output_adapter_piece = jnp.sum(
        jnp.where(membership[:, :, None], request_output_factors, 0.0), axis=1
    )
    result_lowrank_source = sum_mp(output_adapter_piece).astype(jnp.bfloat16)
    result_seat_lines = result_lowrank_right.shape[0]
    output_slots = mp_index * result_seat_lines + jnp.arange(result_seat_lines, dtype=jnp.int32)
    resident_here = (token_adapter_slot[:, None] == output_slots[None, :]).astype(jnp.bfloat16)
    broadened_result = (resident_here[:, :, None] * result_lowrank_source[:, None, :]).reshape(
        prompt_ordinal, result_seat_lines * LOW_DIMENSION
    )
    raised_window = result_lowrank_right.reshape(result_seat_lines * LOW_DIMENSION, HIDDEN_BREADTH)
    attn_sum = scatter_mp(
        (
            jnp.dot(attended, output_weight, preferred_element_type=jnp.float32)
            + jnp.dot(broadened_result, raised_window, preferred_element_type=jnp.float32)
        ).astype(jnp.bfloat16)
    ).astype(jnp.float32)
    after_attn = (residual + rms_scale(attn_sum, after_attention_gain)).astype(jnp.bfloat16)
    normed_ffw = rms_scale(after_attn.astype(jnp.float32), before_feedforward_gain).astype(
        jnp.bfloat16
    )
    piece = gather_mp(normed_ffw)
    gated = jnp.dot(piece, gate_matrix, preferred_element_type=jnp.float32)
    upward = jnp.dot(piece, up_matrix, preferred_element_type=jnp.float32)
    hidden = (jax.nn.gelu(gated, approximate=True) * upward).astype(jnp.bfloat16)
    ffw_sum = scatter_mp(
        jnp.dot(hidden, down_matrix, preferred_element_type=jnp.float32).astype(jnp.bfloat16)
    ).astype(jnp.float32)
    hidden_out = (
        after_attn.astype(jnp.float32) + rms_scale(ffw_sum, after_feedforward_gain)
    ).astype(jnp.bfloat16)
    return (hidden_out, kv_new)


def solution(mesh):
    fine_mesh = jax.sharding.Mesh(
        mesh.devices.reshape(2, 2, 4, 4, 2), DP_AXES + MP_AXES
    )
    return jax.shard_map(
        shards,
        mesh=fine_mesh,
        in_specs=(
            P(DP_AXES + MP_AXES, None),
            P(),
            P(),
            P(),
            P(),
            P(None, MP_AXES),
            P(None, None, MP_AXES, None),
            P(MP_AXES, None),
            P(None, MP_AXES),
            P(None, MP_AXES),
            P(MP_AXES, None),
            P(DP_AXES, None, MP_AXES, None, None),
            P(MP_AXES, None, None),
            P(None, None, None, MP_AXES, None),
            P(None, MP_AXES, None),
            P(MP_AXES, None, None),
            P(DP_AXES, None),
            P(DP_AXES, None),
            P(),
            P(),
        ),
        out_specs=(P(DP_AXES + MP_AXES, None), P(DP_AXES, None, MP_AXES, None)),
        check_vma=False,
    )
```

```python
import math

import jax
import jax.numpy as jnp
from jax import lax
from jax.sharding import PartitionSpec as P

HIDDEN_BREADTH = 4608
ASKING_CHANNELS = 32
CHANNEL_LENGTH = 128
NUM_LOW_TERMS = 64
LOW_DIMENSION = 16
SHARD_PROMPTS = 8
PPR = 4
PAGE = 16


EPS = 1e-06
SOFTCAP = 50.0

DP_AXES = ("zh", "c")
MP_AXES = ("x", "y", "zl")


AXIS_SIZES = {"zh": 2, "c": 2, "x": 4, "y": 4, "zl": 2}
PAIR_SWAP = ((0, 1), (1, 0))


PLANE_FLOWS = (("x", 1), ("x", -1), ("y", 1), ("y", -1))


def ring_gather(block, name, direction):
    size = AXIS_SIZES[name]
    me = lax.axis_index(name)
    perm = [(i, (i + direction) % size) for i in range(size)]
    gathered = jnp.zeros((size,) + block.shape, block.dtype)
    gathered = lax.dynamic_update_index_in_dim(gathered, block, me, 0)
    moving = block
    for step in range(size - 1):
        moving = lax.ppermute(moving, name, perm=perm)
        source = jnp.remainder(me - direction * (step + 1), size)
        gathered = lax.dynamic_update_index_in_dim(gathered, moving, source, 0)
    return gathered


def ring_scatter(blocks, name, direction):
    size = AXIS_SIZES[name]
    me = lax.axis_index(name)
    perm = [(i, (i + direction) % size) for i in range(size)]

    def own(offset):
        index = jnp.remainder(me + offset, size)
        return lax.dynamic_index_in_dim(blocks, index, 0, keepdims=False).astype(jnp.float32)

    moving = own(-direction).astype(blocks.dtype)
    for step in range(size - 1):
        arrived = lax.ppermute(moving, name, perm=perm).astype(jnp.float32)
        if step < size - 2:
            moving = (arrived + own(-direction * (step + 2))).astype(blocks.dtype)
    return arrived + own(0)


def gather_plane(values):
    quarter = values.shape[-1] // len(PLANE_FLOWS)
    pieces = []
    for index, (first, direction) in enumerate(PLANE_FLOWS):
        part = values[:, index * quarter:(index + 1) * quarter]
        if first == "x":
            part = ring_gather(ring_gather(part, "y", direction), "x", direction)
        else:
            part = jnp.swapaxes(ring_gather(ring_gather(part, "x", direction), "y", direction), 0, 1)
        pieces.append(part.reshape(-1, quarter))
    return jnp.concatenate(pieces, axis=-1)


def scatter_plane(values):
    quarter = values.shape[-1] // len(PLANE_FLOWS)
    rows = values.reshape(AXIS_SIZES["x"], AXIS_SIZES["y"], -1, values.shape[-1])
    pieces = []
    for index, (first, direction) in enumerate(PLANE_FLOWS):
        part = rows[..., index * quarter:(index + 1) * quarter]
        if first == "x":
            part = ring_scatter(part, "x", direction).astype(values.dtype)
            part = ring_scatter(part, "y", direction)
        else:
            part = ring_scatter(jnp.swapaxes(part, 0, 1), "y", direction).astype(values.dtype)
            part = ring_scatter(part, "x", direction)
        pieces.append(part)
    return jnp.concatenate(pieces, axis=-1)


def gather_mp(values):
    other = lax.ppermute(values, "zl", perm=PAIR_SWAP)
    lead = lax.axis_index("zl") == 0
    values = jnp.concatenate(
        [jnp.where(lead, values, other), jnp.where(lead, other, values)], axis=0
    )
    return lax.all_gather(values, ("x", "y"), axis=0, tiled=True)


def scatter_mp(values):
    values = scatter_plane(values)
    half = values.shape[0] // 2
    lead = lax.axis_index("zl") == 0
    keep = jnp.where(lead, values[:half], values[half:])
    send = jnp.where(lead, values[half:], values[:half]).astype(jnp.bfloat16)
    other = lax.ppermute(send, "zl", perm=PAIR_SWAP)
    return keep + other.astype(jnp.float32)


def sum_mp(values):
    for name in ("zl", "y", "x"):
        step = 1
        while step < AXIS_SIZES[name]:
            partner = [(i, i ^ step) for i in range(AXIS_SIZES[name])]
            values = values + lax.ppermute(values, name, perm=partner)
            step *= 2
    return values


def rms_scale(values, scaling):
    mean_square = jnp.mean(values * values, axis=-1, keepdims=True)
    return values * lax.rsqrt(mean_square + EPS) * scaling


def apply_rotary(values, token_positions):
    half_dim = values.shape[-1] // 2
    frequency = 10000.0 ** (-2.0 * jnp.arange(half_dim, dtype=jnp.float32) / values.shape[-1])
    angles = token_positions.astype(jnp.float32)[:, None] * frequency[None, :]
    cosine = jnp.cos(angles)[:, None, :]
    sine_part = jnp.sin(angles)[:, None, :]
    first_half = values[..., :half_dim]
    second_half = values[..., half_dim:]
    return jnp.concatenate(
        [
            first_half * cosine - second_half * sine_part,
            second_half * cosine + first_half * sine_part,
        ],
        axis=-1,
    )


def positions_of(segments):
    length = segments.shape[0]
    earlier = jnp.sum((segments[None, :] < segments[:, None]).astype(jnp.int32), axis=1)
    return PPR * PAGE + jnp.arange(length, dtype=jnp.int32) - earlier


def capped(scores):
    return SOFTCAP * jnp.tanh(scores / SOFTCAP)


def attend_local(query_rows, keys_new, fresh_values, keys_pre, values_pre, segments):
    scale_factor = 1.0 / math.sqrt(HIDDEN_BREADTH // ASKING_CHANNELS)
    length = segments.shape[0]
    prefix_owner = jnp.arange(keys_pre.shape[1], dtype=jnp.int32) // (PPR * PAGE)
    mask_pre = (prefix_owner[None, :] == segments[:, None])[None]
    ordinal = jnp.arange(length, dtype=jnp.int32)
    mask_new = ((segments[None, :] == segments[:, None]) & (ordinal[None, :] <= ordinal[:, None]))[
        None
    ]
    scores_pre = (
        jnp.einsum("thd,hjd->htj", query_rows, keys_pre, preferred_element_type=jnp.float32)
        * scale_factor
    )
    scores_new = (
        jnp.einsum("thd,uhd->htu", query_rows, keys_new, preferred_element_type=jnp.float32)
        * scale_factor
    )
    weight_pre = jnp.where(mask_pre, jnp.exp(capped(scores_pre)), 0.0)
    weight_new = jnp.where(mask_new, jnp.exp(capped(scores_new)), 0.0)
    totals = jnp.sum(weight_pre, axis=-1, keepdims=True) + jnp.sum(
        weight_new, axis=-1, keepdims=True
    )
    probs_pre = (weight_pre / totals).astype(jnp.bfloat16)
    probs_new = (weight_new / totals).astype(jnp.bfloat16)
    mixture = jnp.einsum("htj,hjd->thd", probs_pre, values_pre, preferred_element_type=jnp.float32)
    mixture = mixture + jnp.einsum(
        "htu,uhd->thd", probs_new, fresh_values, preferred_element_type=jnp.float32
    )
    return mixture.astype(jnp.bfloat16).reshape(length, -1)


def shards(
    residual_input,
    before_attention_gain,
    after_attention_gain,
    before_feedforward_gain,
    after_feedforward_gain,
    query_weight,
    key_value_weight,
    output_weight,
    gate_matrix,
    up_matrix,
    down_matrix,
    key_value_cache,
    projected_lowrank_left,
    projected_lowrank_right,
    result_lowrank_left,
    result_lowrank_right,
    token_request,
    lowrank_choice_by_prompt,
    adapter_position,
    request_pages,
):
    mp_index = lax.axis_index(MP_AXES)
    dp_index = lax.axis_index(DP_AXES)
    residual = residual_input.astype(jnp.float32)
    normed_rows = rms_scale(residual, before_attention_gain).astype(jnp.bfloat16)
    normalized_rows = gather_mp(normed_rows)
    prompt_ordinal = normalized_rows.shape[0]
    channel_window = query_weight.shape[1] // CHANNEL_LENGTH
    query_rows = jnp.dot(normalized_rows, query_weight, preferred_element_type=jnp.float32).reshape(
        prompt_ordinal, channel_window, CHANNEL_LENGTH
    )
    key_value_rows = jnp.dot(
        normalized_rows,
        key_value_weight.reshape(HIDDEN_BREADTH, 2 * channel_window * CHANNEL_LENGTH),
        preferred_element_type=jnp.float32,
    ).reshape(prompt_ordinal, 2, channel_window, CHANNEL_LENGTH)
    segments = token_request[0]
    request_ids = lowrank_choice_by_prompt[0]
    request_range = jnp.arange(SHARD_PROMPTS, dtype=jnp.int32)
    membership = segments[:, None] == request_range[None, :]
    adapter_range = jnp.arange(NUM_LOW_TERMS, dtype=jnp.int32)
    token_adapter = jnp.sum(jnp.where(membership, request_ids[None, :], 0), axis=1)
    token_adapter_slot = jnp.sum(
        jnp.where(token_adapter[:, None] == adapter_range[None, :], adapter_position[None, :], 0),
        axis=1,
    )
    seat_count = projected_lowrank_left.shape[0]
    local_seats = mp_index * seat_count + jnp.arange(seat_count, dtype=jnp.int32)
    seat_factors = jnp.einsum(
        "td,sdk->tsk", normalized_rows, projected_lowrank_left, preferred_element_type=jnp.float32
    )
    seat_here = token_adapter_slot[:, None] == local_seats[None, :]
    lowrank_source = jnp.sum(jnp.where(seat_here[:, :, None], seat_factors, 0.0), axis=1)
    lowrank_source = sum_mp(lowrank_source).astype(jnp.bfloat16)
    choice_mask_table = membership.astype(jnp.bfloat16)
    broadened_lines = (choice_mask_table[:, :, None] * lowrank_source[:, None, :]).reshape(
        prompt_ordinal, SHARD_PROMPTS * LOW_DIMENSION
    )
    raised_result_lines = projected_lowrank_right[request_ids].reshape(
        SHARD_PROMPTS * LOW_DIMENSION, 3 * channel_window * CHANNEL_LENGTH
    )
    adapter_query_key_value = jnp.dot(
        broadened_lines, raised_result_lines, preferred_element_type=jnp.float32
    ).reshape(prompt_ordinal, 3, channel_window, CHANNEL_LENGTH)
    token_positions = positions_of(segments)
    rotary_queries = apply_rotary(
        query_rows + adapter_query_key_value[:, 0], token_positions
    ).astype(jnp.bfloat16)
    rotary_keys = apply_rotary(
        key_value_rows[:, 0] + adapter_query_key_value[:, 1], token_positions
    ).astype(jnp.bfloat16)
    fresh_values = (key_value_rows[:, 1] + adapter_query_key_value[:, 2]).astype(jnp.bfloat16)
    kv_new = jnp.stack([rotary_keys, fresh_values], axis=1)
    own_pages = lax.dynamic_index_in_dim(request_pages, dp_index, 0, keepdims=False).reshape(
        SHARD_PROMPTS * PPR
    )
    whole_pool = lax.all_gather(key_value_cache, DP_AXES, axis=0, tiled=True)
    chosen = whole_pool[own_pages]
    keys_pre = jnp.transpose(chosen[:, 0], (1, 0, 2, 3)).reshape(
        channel_window, SHARD_PROMPTS * PPR * PAGE, CHANNEL_LENGTH
    )
    values_pre = jnp.transpose(chosen[:, 1], (1, 0, 2, 3)).reshape(
        channel_window, SHARD_PROMPTS * PPR * PAGE, CHANNEL_LENGTH
    )
    attended = attend_local(
        rotary_queries, rotary_keys, fresh_values, keys_pre, values_pre, segments
    )
    request_output_down = result_lowrank_left[request_ids]
    request_output_factors = jnp.einsum(
        "tc,rck->trk", attended, request_output_down, preferred_element_type=jnp.float32
    )
    output_adapter_piece = jnp.sum(
        jnp.where(membership[:, :, None], request_output_factors, 0.0), axis=1
    )
    result_lowrank_source = sum_mp(output_adapter_piece).astype(jnp.bfloat16)
    result_seat_lines = result_lowrank_right.shape[0]
    output_slots = mp_index * result_seat_lines + jnp.arange(result_seat_lines, dtype=jnp.int32)
    resident_here = (token_adapter_slot[:, None] == output_slots[None, :]).astype(jnp.bfloat16)
    broadened_result = (resident_here[:, :, None] * result_lowrank_source[:, None, :]).reshape(
        prompt_ordinal, result_seat_lines * LOW_DIMENSION
    )
    raised_window = result_lowrank_right.reshape(result_seat_lines * LOW_DIMENSION, HIDDEN_BREADTH)
    attn_sum = scatter_mp(
        (
            jnp.dot(attended, output_weight, preferred_element_type=jnp.float32)
            + jnp.dot(broadened_result, raised_window, preferred_element_type=jnp.float32)
        ).astype(jnp.bfloat16)
    ).astype(jnp.float32)
    after_attn = (residual + rms_scale(attn_sum, after_attention_gain)).astype(jnp.bfloat16)
    normed_ffw = rms_scale(after_attn.astype(jnp.float32), before_feedforward_gain).astype(
        jnp.bfloat16
    )
    piece = gather_mp(normed_ffw)
    gated = jnp.dot(piece, gate_matrix, preferred_element_type=jnp.float32)
    upward = jnp.dot(piece, up_matrix, preferred_element_type=jnp.float32)
    hidden = (jax.nn.gelu(gated, approximate=True) * upward).astype(jnp.bfloat16)
    ffw_sum = scatter_mp(
        jnp.dot(hidden, down_matrix, preferred_element_type=jnp.float32).astype(jnp.bfloat16)
    ).astype(jnp.float32)
    hidden_out = (
        after_attn.astype(jnp.float32) + rms_scale(ffw_sum, after_feedforward_gain)
    ).astype(jnp.bfloat16)
    return (hidden_out, kv_new)


def solution(mesh):
    fine_mesh = jax.sharding.Mesh(
        mesh.devices.reshape(2, 2, 4, 4, 2), DP_AXES + MP_AXES
    )
    return jax.shard_map(
        shards,
        mesh=fine_mesh,
        in_specs=(
            P(DP_AXES + MP_AXES, None),
            P(),
            P(),
            P(),
            P(),
            P(None, MP_AXES),
            P(None, None, MP_AXES, None),
            P(MP_AXES, None),
            P(None, MP_AXES),
            P(None, MP_AXES),
            P(MP_AXES, None),
            P(DP_AXES, None, MP_AXES, None, None),
            P(MP_AXES, None, None),
            P(None, None, None, MP_AXES, None),
            P(None, MP_AXES, None),
            P(MP_AXES, None, None),
            P(DP_AXES, None),
            P(DP_AXES, None),
            P(),
            P(),
        ),
        out_specs=(P(DP_AXES + MP_AXES, None), P(DP_AXES, None, MP_AXES, None)),
        check_vma=False,
    )
```

```python
import math

import jax
import jax.numpy as jnp
from jax import lax
from jax.sharding import PartitionSpec as P

HIDDEN_BREADTH = 4608
ASKING_CHANNELS = 32
CHANNEL_LENGTH = 128
NUM_LOW_TERMS = 64
LOW_DIMENSION = 16
SHARD_PROMPTS = 8
PPR = 4
PAGE = 16


EPS = 1e-06
SOFTCAP = 50.0

DP_AXES = ("zh", "c")
MP_AXES = ("x", "y", "zl")


AXIS_SIZES = {"zh": 2, "c": 2, "x": 4, "y": 4, "zl": 2}
PAIR_SWAP = ((0, 1), (1, 0))


PLANE_FLOWS = (("x", 1), ("x", -1), ("y", 1), ("y", -1))


def ring_gather(block, name, direction):
    size = AXIS_SIZES[name]
    me = lax.axis_index(name)
    perm = [(i, (i + direction) % size) for i in range(size)]
    gathered = jnp.zeros((size,) + block.shape, block.dtype)
    gathered = lax.dynamic_update_index_in_dim(gathered, block, me, 0)
    moving = block
    for step in range(size - 1):
        moving = lax.ppermute(moving, name, perm=perm)
        source = jnp.remainder(me - direction * (step + 1), size)
        gathered = lax.dynamic_update_index_in_dim(gathered, moving, source, 0)
    return gathered


def ring_scatter(blocks, name, direction):
    size = AXIS_SIZES[name]
    me = lax.axis_index(name)
    perm = [(i, (i + direction) % size) for i in range(size)]

    def own(offset):
        index = jnp.remainder(me + offset, size)
        return lax.dynamic_index_in_dim(blocks, index, 0, keepdims=False).astype(jnp.float32)

    moving = own(-direction).astype(blocks.dtype)
    for step in range(size - 1):
        arrived = lax.ppermute(moving, name, perm=perm).astype(jnp.float32)
        if step < size - 2:
            moving = (arrived + own(-direction * (step + 2))).astype(blocks.dtype)
    return arrived + own(0)


def gather_plane(values):
    quarter = values.shape[-1] // len(PLANE_FLOWS)
    pieces = []
    for index, (first, direction) in enumerate(PLANE_FLOWS):
        part = values[:, index * quarter:(index + 1) * quarter]
        if first == "x":
            part = ring_gather(ring_gather(part, "y", direction), "x", direction)
        else:
            part = jnp.swapaxes(ring_gather(ring_gather(part, "x", direction), "y", direction), 0, 1)
        pieces.append(part.reshape(-1, quarter))
    return jnp.concatenate(pieces, axis=-1)


def scatter_plane(values):
    quarter = values.shape[-1] // len(PLANE_FLOWS)
    rows = values.reshape(AXIS_SIZES["x"], AXIS_SIZES["y"], -1, values.shape[-1])
    pieces = []
    for index, (first, direction) in enumerate(PLANE_FLOWS):
        part = rows[..., index * quarter:(index + 1) * quarter]
        if first == "x":
            part = ring_scatter(part, "x", direction).astype(values.dtype)
            part = ring_scatter(part, "y", direction)
        else:
            part = ring_scatter(jnp.swapaxes(part, 0, 1), "y", direction).astype(values.dtype)
            part = ring_scatter(part, "x", direction)
        pieces.append(part)
    return jnp.concatenate(pieces, axis=-1)


def gather_mp(values):
    other = lax.ppermute(values, "zl", perm=PAIR_SWAP)
    lead = lax.axis_index("zl") == 0
    values = jnp.concatenate(
        [jnp.where(lead, values, other), jnp.where(lead, other, values)], axis=0
    )
    return gather_plane(values)


def scatter_mp(values):
    plane = AXIS_SIZES["x"] * AXIS_SIZES["y"]
    values = lax.all_to_all(values, ("x", "y"), 0, 0, tiled=True)
    values = jnp.sum(
        values.reshape(plane, -1, values.shape[-1]).astype(jnp.float32), axis=0
    )
    half = values.shape[0] // 2
    lead = lax.axis_index("zl") == 0
    keep = jnp.where(lead, values[:half], values[half:])
    send = jnp.where(lead, values[half:], values[:half]).astype(jnp.bfloat16)
    other = lax.ppermute(send, "zl", perm=PAIR_SWAP)
    return keep + other.astype(jnp.float32)


def sum_mp(values):
    for name in ("zl", "y", "x"):
        step = 1
        while step < AXIS_SIZES[name]:
            partner = [(i, i ^ step) for i in range(AXIS_SIZES[name])]
            values = values + lax.ppermute(values, name, perm=partner)
            step *= 2
    return values


def rms_scale(values, scaling):
    mean_square = jnp.mean(values * values, axis=-1, keepdims=True)
    return values * lax.rsqrt(mean_square + EPS) * scaling


def apply_rotary(values, token_positions):
    half_dim = values.shape[-1] // 2
    frequency = 10000.0 ** (-2.0 * jnp.arange(half_dim, dtype=jnp.float32) / values.shape[-1])
    angles = token_positions.astype(jnp.float32)[:, None] * frequency[None, :]
    cosine = jnp.cos(angles)[:, None, :]
    sine_part = jnp.sin(angles)[:, None, :]
    first_half = values[..., :half_dim]
    second_half = values[..., half_dim:]
    return jnp.concatenate(
        [
            first_half * cosine - second_half * sine_part,
            second_half * cosine + first_half * sine_part,
        ],
        axis=-1,
    )


def positions_of(segments):
    length = segments.shape[0]
    earlier = jnp.sum((segments[None, :] < segments[:, None]).astype(jnp.int32), axis=1)
    return PPR * PAGE + jnp.arange(length, dtype=jnp.int32) - earlier


def capped(scores):
    return SOFTCAP * jnp.tanh(scores / SOFTCAP)


def attend_local(query_rows, keys_new, fresh_values, keys_pre, values_pre, segments):
    scale_factor = 1.0 / math.sqrt(HIDDEN_BREADTH // ASKING_CHANNELS)
    length = segments.shape[0]
    prefix_owner = jnp.arange(keys_pre.shape[1], dtype=jnp.int32) // (PPR * PAGE)
    mask_pre = (prefix_owner[None, :] == segments[:, None])[None]
    ordinal = jnp.arange(length, dtype=jnp.int32)
    mask_new = ((segments[None, :] == segments[:, None]) & (ordinal[None, :] <= ordinal[:, None]))[
        None
    ]
    scores_pre = (
        jnp.einsum("thd,hjd->htj", query_rows, keys_pre, preferred_element_type=jnp.float32)
        * scale_factor
    )
    scores_new = (
        jnp.einsum("thd,uhd->htu", query_rows, keys_new, preferred_element_type=jnp.float32)
        * scale_factor
    )
    weight_pre = jnp.where(mask_pre, jnp.exp(capped(scores_pre)), 0.0)
    weight_new = jnp.where(mask_new, jnp.exp(capped(scores_new)), 0.0)
    totals = jnp.sum(weight_pre, axis=-1, keepdims=True) + jnp.sum(
        weight_new, axis=-1, keepdims=True
    )
    probs_pre = (weight_pre / totals).astype(jnp.bfloat16)
    probs_new = (weight_new / totals).astype(jnp.bfloat16)
    mixture = jnp.einsum("htj,hjd->thd", probs_pre, values_pre, preferred_element_type=jnp.float32)
    mixture = mixture + jnp.einsum(
        "htu,uhd->thd", probs_new, fresh_values, preferred_element_type=jnp.float32
    )
    return mixture.astype(jnp.bfloat16).reshape(length, -1)


def shards(
    residual_input,
    before_attention_gain,
    after_attention_gain,
    before_feedforward_gain,
    after_feedforward_gain,
    query_weight,
    key_value_weight,
    output_weight,
    gate_matrix,
    up_matrix,
    down_matrix,
    key_value_cache,
    projected_lowrank_left,
    projected_lowrank_right,
    result_lowrank_left,
    result_lowrank_right,
    token_request,
    lowrank_choice_by_prompt,
    adapter_position,
    request_pages,
):
    mp_index = lax.axis_index(MP_AXES)
    dp_index = lax.axis_index(DP_AXES)
    residual = residual_input.astype(jnp.float32)
    normed_rows = rms_scale(residual, before_attention_gain).astype(jnp.bfloat16)
    normalized_rows = gather_mp(normed_rows)
    prompt_ordinal = normalized_rows.shape[0]
    channel_window = query_weight.shape[1] // CHANNEL_LENGTH
    query_rows = jnp.dot(normalized_rows, query_weight, preferred_element_type=jnp.float32).reshape(
        prompt_ordinal, channel_window, CHANNEL_LENGTH
    )
    key_value_rows = jnp.dot(
        normalized_rows,
        key_value_weight.reshape(HIDDEN_BREADTH, 2 * channel_window * CHANNEL_LENGTH),
        preferred_element_type=jnp.float32,
    ).reshape(prompt_ordinal, 2, channel_window, CHANNEL_LENGTH)
    segments = token_request[0]
    request_ids = lowrank_choice_by_prompt[0]
    request_range = jnp.arange(SHARD_PROMPTS, dtype=jnp.int32)
    membership = segments[:, None] == request_range[None, :]
    adapter_range = jnp.arange(NUM_LOW_TERMS, dtype=jnp.int32)
    token_adapter = jnp.sum(jnp.where(membership, request_ids[None, :], 0), axis=1)
    token_adapter_slot = jnp.sum(
        jnp.where(token_adapter[:, None] == adapter_range[None, :], adapter_position[None, :], 0),
        axis=1,
    )
    seat_count = projected_lowrank_left.shape[0]
    local_seats = mp_index * seat_count + jnp.arange(seat_count, dtype=jnp.int32)
    seat_factors = jnp.einsum(
        "td,sdk->tsk", normalized_rows, projected_lowrank_left, preferred_element_type=jnp.float32
    )
    seat_here = token_adapter_slot[:, None] == local_seats[None, :]
    lowrank_source = jnp.sum(jnp.where(seat_here[:, :, None], seat_factors, 0.0), axis=1)
    lowrank_source = sum_mp(lowrank_source).astype(jnp.bfloat16)
    choice_mask_table = membership.astype(jnp.bfloat16)
    broadened_lines = (choice_mask_table[:, :, None] * lowrank_source[:, None, :]).reshape(
        prompt_ordinal, SHARD_PROMPTS * LOW_DIMENSION
    )
    raised_result_lines = projected_lowrank_right[request_ids].reshape(
        SHARD_PROMPTS * LOW_DIMENSION, 3 * channel_window * CHANNEL_LENGTH
    )
    adapter_query_key_value = jnp.dot(
        broadened_lines, raised_result_lines, preferred_element_type=jnp.float32
    ).reshape(prompt_ordinal, 3, channel_window, CHANNEL_LENGTH)
    token_positions = positions_of(segments)
    rotary_queries = apply_rotary(
        query_rows + adapter_query_key_value[:, 0], token_positions
    ).astype(jnp.bfloat16)
    rotary_keys = apply_rotary(
        key_value_rows[:, 0] + adapter_query_key_value[:, 1], token_positions
    ).astype(jnp.bfloat16)
    fresh_values = (key_value_rows[:, 1] + adapter_query_key_value[:, 2]).astype(jnp.bfloat16)
    kv_new = jnp.stack([rotary_keys, fresh_values], axis=1)
    own_pages = lax.dynamic_index_in_dim(request_pages, dp_index, 0, keepdims=False).reshape(
        SHARD_PROMPTS * PPR
    )
    whole_pool = lax.all_gather(key_value_cache, DP_AXES, axis=0, tiled=True)
    chosen = whole_pool[own_pages]
    keys_pre = jnp.transpose(chosen[:, 0], (1, 0, 2, 3)).reshape(
        channel_window, SHARD_PROMPTS * PPR * PAGE, CHANNEL_LENGTH
    )
    values_pre = jnp.transpose(chosen[:, 1], (1, 0, 2, 3)).reshape(
        channel_window, SHARD_PROMPTS * PPR * PAGE, CHANNEL_LENGTH
    )
    attended = attend_local(
        rotary_queries, rotary_keys, fresh_values, keys_pre, values_pre, segments
    )
    request_output_down = result_lowrank_left[request_ids]
    request_output_factors = jnp.einsum(
        "tc,rck->trk", attended, request_output_down, preferred_element_type=jnp.float32
    )
    output_adapter_piece = jnp.sum(
        jnp.where(membership[:, :, None], request_output_factors, 0.0), axis=1
    )
    result_lowrank_source = sum_mp(output_adapter_piece).astype(jnp.bfloat16)
    result_seat_lines = result_lowrank_right.shape[0]
    output_slots = mp_index * result_seat_lines + jnp.arange(result_seat_lines, dtype=jnp.int32)
    resident_here = (token_adapter_slot[:, None] == output_slots[None, :]).astype(jnp.bfloat16)
    broadened_result = (resident_here[:, :, None] * result_lowrank_source[:, None, :]).reshape(
        prompt_ordinal, result_seat_lines * LOW_DIMENSION
    )
    raised_window = result_lowrank_right.reshape(result_seat_lines * LOW_DIMENSION, HIDDEN_BREADTH)
    attn_sum = scatter_mp(
        (
            jnp.dot(attended, output_weight, preferred_element_type=jnp.float32)
            + jnp.dot(broadened_result, raised_window, preferred_element_type=jnp.float32)
        ).astype(jnp.bfloat16)
    ).astype(jnp.float32)
    after_attn = (residual + rms_scale(attn_sum, after_attention_gain)).astype(jnp.bfloat16)
    normed_ffw = rms_scale(after_attn.astype(jnp.float32), before_feedforward_gain).astype(
        jnp.bfloat16
    )
    piece = gather_mp(normed_ffw)
    gated = jnp.dot(piece, gate_matrix, preferred_element_type=jnp.float32)
    upward = jnp.dot(piece, up_matrix, preferred_element_type=jnp.float32)
    hidden = (jax.nn.gelu(gated, approximate=True) * upward).astype(jnp.bfloat16)
    ffw_sum = scatter_mp(
        jnp.dot(hidden, down_matrix, preferred_element_type=jnp.float32).astype(jnp.bfloat16)
    ).astype(jnp.float32)
    hidden_out = (
        after_attn.astype(jnp.float32) + rms_scale(ffw_sum, after_feedforward_gain)
    ).astype(jnp.bfloat16)
    return (hidden_out, kv_new)


def solution(mesh):
    fine_mesh = jax.sharding.Mesh(
        mesh.devices.reshape(2, 2, 4, 4, 2), DP_AXES + MP_AXES
    )
    return jax.shard_map(
        shards,
        mesh=fine_mesh,
        in_specs=(
            P(DP_AXES + MP_AXES, None),
            P(),
            P(),
            P(),
            P(),
            P(None, MP_AXES),
            P(None, None, MP_AXES, None),
            P(MP_AXES, None),
            P(None, MP_AXES),
            P(None, MP_AXES),
            P(MP_AXES, None),
            P(DP_AXES, None, MP_AXES, None, None),
            P(MP_AXES, None, None),
            P(None, None, None, MP_AXES, None),
            P(None, MP_AXES, None),
            P(MP_AXES, None, None),
            P(DP_AXES, None),
            P(DP_AXES, None),
            P(),
            P(),
        ),
        out_specs=(P(DP_AXES + MP_AXES, None), P(DP_AXES, None, MP_AXES, None)),
        check_vma=False,
    )
```

```python
import math

import jax
import jax.numpy as jnp
from jax import lax
from jax.sharding import PartitionSpec as P

HIDDEN_BREADTH = 4608
ASKING_CHANNELS = 32
CHANNEL_LENGTH = 128
NUM_LOW_TERMS = 64
LOW_DIMENSION = 16
SHARD_PROMPTS = 8
PPR = 4
PAGE = 16


EPS = 1e-06
SOFTCAP = 50.0

DP_AXES = ("zh", "c")
MP_AXES = ("x", "y", "zl")


AXIS_SIZES = {"zh": 2, "c": 2, "x": 4, "y": 4, "zl": 2}
PAIR_SWAP = ((0, 1), (1, 0))


PLANE_FLOWS = (("x", 1), ("x", -1), ("y", 1), ("y", -1))


def ring_gather(block, name, direction):
    size = AXIS_SIZES[name]
    me = lax.axis_index(name)
    perm = [(i, (i + direction) % size) for i in range(size)]
    gathered = jnp.zeros((size,) + block.shape, block.dtype)
    gathered = lax.dynamic_update_index_in_dim(gathered, block, me, 0)
    moving = block
    for step in range(size - 1):
        moving = lax.ppermute(moving, name, perm=perm)
        source = jnp.remainder(me - direction * (step + 1), size)
        gathered = lax.dynamic_update_index_in_dim(gathered, moving, source, 0)
    return gathered


def ring_scatter(blocks, name, direction):
    size = AXIS_SIZES[name]
    me = lax.axis_index(name)
    perm = [(i, (i + direction) % size) for i in range(size)]

    def own(offset):
        index = jnp.remainder(me + offset, size)
        return lax.dynamic_index_in_dim(blocks, index, 0, keepdims=False).astype(jnp.float32)

    moving = own(-direction).astype(blocks.dtype)
    for step in range(size - 1):
        arrived = lax.ppermute(moving, name, perm=perm).astype(jnp.float32)
        if step < size - 2:
            moving = (arrived + own(-direction * (step + 2))).astype(blocks.dtype)
    return arrived + own(0)


def gather_plane(values):
    quarter = values.shape[-1] // len(PLANE_FLOWS)
    pieces = []
    for index, (first, direction) in enumerate(PLANE_FLOWS):
        part = values[:, index * quarter:(index + 1) * quarter]
        if first == "x":
            part = ring_gather(ring_gather(part, "y", direction), "x", direction)
        else:
            part = jnp.swapaxes(ring_gather(ring_gather(part, "x", direction), "y", direction), 0, 1)
        pieces.append(part.reshape(-1, quarter))
    return jnp.concatenate(pieces, axis=-1)


def scatter_plane(values):
    quarter = values.shape[-1] // len(PLANE_FLOWS)
    rows = values.reshape(AXIS_SIZES["x"], AXIS_SIZES["y"], -1, values.shape[-1])
    pieces = []
    for index, (first, direction) in enumerate(PLANE_FLOWS):
        part = rows[..., index * quarter:(index + 1) * quarter]
        if first == "x":
            part = ring_scatter(part, "x", direction).astype(values.dtype)
            part = ring_scatter(part, "y", direction)
        else:
            part = ring_scatter(jnp.swapaxes(part, 0, 1), "y", direction).astype(values.dtype)
            part = ring_scatter(part, "x", direction)
        pieces.append(part)
    return jnp.concatenate(pieces, axis=-1)


def gather_mp(values):
    other = lax.ppermute(values, "zl", perm=PAIR_SWAP)
    lead = lax.axis_index("zl") == 0
    values = jnp.concatenate(
        [jnp.where(lead, values, other), jnp.where(lead, other, values)], axis=0
    )
    plane = AXIS_SIZES["x"] * AXIS_SIZES["y"]
    copies = jnp.broadcast_to(values[None], (plane,) + values.shape)
    gathered = lax.all_to_all(copies, ("x", "y"), 0, 0, tiled=True)
    return gathered.reshape(-1, values.shape[-1])


def scatter_mp(values):
    plane = AXIS_SIZES["x"] * AXIS_SIZES["y"]
    values = lax.all_to_all(values, ("x", "y"), 0, 0, tiled=True)
    values = jnp.sum(
        values.reshape(plane, -1, values.shape[-1]).astype(jnp.float32), axis=0
    )
    half = values.shape[0] // 2
    lead = lax.axis_index("zl") == 0
    keep = jnp.where(lead, values[:half], values[half:])
    send = jnp.where(lead, values[half:], values[:half]).astype(jnp.bfloat16)
    other = lax.ppermute(send, "zl", perm=PAIR_SWAP)
    return keep + other.astype(jnp.float32)


def sum_mp(values):
    for name in ("zl", "y", "x"):
        step = 1
        while step < AXIS_SIZES[name]:
            partner = [(i, i ^ step) for i in range(AXIS_SIZES[name])]
            values = values + lax.ppermute(values, name, perm=partner)
            step *= 2
    return values


def rms_scale(values, scaling):
    mean_square = jnp.mean(values * values, axis=-1, keepdims=True)
    return values * lax.rsqrt(mean_square + EPS) * scaling


def apply_rotary(values, token_positions):
    half_dim = values.shape[-1] // 2
    frequency = 10000.0 ** (-2.0 * jnp.arange(half_dim, dtype=jnp.float32) / values.shape[-1])
    angles = token_positions.astype(jnp.float32)[:, None] * frequency[None, :]
    cosine = jnp.cos(angles)[:, None, :]
    sine_part = jnp.sin(angles)[:, None, :]
    first_half = values[..., :half_dim]
    second_half = values[..., half_dim:]
    return jnp.concatenate(
        [
            first_half * cosine - second_half * sine_part,
            second_half * cosine + first_half * sine_part,
        ],
        axis=-1,
    )


def positions_of(segments):
    length = segments.shape[0]
    earlier = jnp.sum((segments[None, :] < segments[:, None]).astype(jnp.int32), axis=1)
    return PPR * PAGE + jnp.arange(length, dtype=jnp.int32) - earlier


def capped(scores):
    return SOFTCAP * jnp.tanh(scores / SOFTCAP)


def attend_local(query_rows, keys_new, fresh_values, keys_pre, values_pre, segments):
    scale_factor = 1.0 / math.sqrt(HIDDEN_BREADTH // ASKING_CHANNELS)
    length = segments.shape[0]
    prefix_owner = jnp.arange(keys_pre.shape[1], dtype=jnp.int32) // (PPR * PAGE)
    mask_pre = (prefix_owner[None, :] == segments[:, None])[None]
    ordinal = jnp.arange(length, dtype=jnp.int32)
    mask_new = ((segments[None, :] == segments[:, None]) & (ordinal[None, :] <= ordinal[:, None]))[
        None
    ]
    scores_pre = (
        jnp.einsum("thd,hjd->htj", query_rows, keys_pre, preferred_element_type=jnp.float32)
        * scale_factor
    )
    scores_new = (
        jnp.einsum("thd,uhd->htu", query_rows, keys_new, preferred_element_type=jnp.float32)
        * scale_factor
    )
    weight_pre = jnp.where(mask_pre, jnp.exp(capped(scores_pre)), 0.0)
    weight_new = jnp.where(mask_new, jnp.exp(capped(scores_new)), 0.0)
    totals = jnp.sum(weight_pre, axis=-1, keepdims=True) + jnp.sum(
        weight_new, axis=-1, keepdims=True
    )
    probs_pre = (weight_pre / totals).astype(jnp.bfloat16)
    probs_new = (weight_new / totals).astype(jnp.bfloat16)
    mixture = jnp.einsum("htj,hjd->thd", probs_pre, values_pre, preferred_element_type=jnp.float32)
    mixture = mixture + jnp.einsum(
        "htu,uhd->thd", probs_new, fresh_values, preferred_element_type=jnp.float32
    )
    return mixture.astype(jnp.bfloat16).reshape(length, -1)


def shards(
    residual_input,
    before_attention_gain,
    after_attention_gain,
    before_feedforward_gain,
    after_feedforward_gain,
    query_weight,
    key_value_weight,
    output_weight,
    gate_matrix,
    up_matrix,
    down_matrix,
    key_value_cache,
    projected_lowrank_left,
    projected_lowrank_right,
    result_lowrank_left,
    result_lowrank_right,
    token_request,
    lowrank_choice_by_prompt,
    adapter_position,
    request_pages,
):
    mp_index = lax.axis_index(MP_AXES)
    dp_index = lax.axis_index(DP_AXES)
    residual = residual_input.astype(jnp.float32)
    normed_rows = rms_scale(residual, before_attention_gain).astype(jnp.bfloat16)
    normalized_rows = gather_mp(normed_rows)
    prompt_ordinal = normalized_rows.shape[0]
    channel_window = query_weight.shape[1] // CHANNEL_LENGTH
    query_rows = jnp.dot(normalized_rows, query_weight, preferred_element_type=jnp.float32).reshape(
        prompt_ordinal, channel_window, CHANNEL_LENGTH
    )
    key_value_rows = jnp.dot(
        normalized_rows,
        key_value_weight.reshape(HIDDEN_BREADTH, 2 * channel_window * CHANNEL_LENGTH),
        preferred_element_type=jnp.float32,
    ).reshape(prompt_ordinal, 2, channel_window, CHANNEL_LENGTH)
    segments = token_request[0]
    request_ids = lowrank_choice_by_prompt[0]
    request_range = jnp.arange(SHARD_PROMPTS, dtype=jnp.int32)
    membership = segments[:, None] == request_range[None, :]
    adapter_range = jnp.arange(NUM_LOW_TERMS, dtype=jnp.int32)
    token_adapter = jnp.sum(jnp.where(membership, request_ids[None, :], 0), axis=1)
    token_adapter_slot = jnp.sum(
        jnp.where(token_adapter[:, None] == adapter_range[None, :], adapter_position[None, :], 0),
        axis=1,
    )
    seat_count = projected_lowrank_left.shape[0]
    local_seats = mp_index * seat_count + jnp.arange(seat_count, dtype=jnp.int32)
    seat_factors = jnp.einsum(
        "td,sdk->tsk", normalized_rows, projected_lowrank_left, preferred_element_type=jnp.float32
    )
    seat_here = token_adapter_slot[:, None] == local_seats[None, :]
    lowrank_source = jnp.sum(jnp.where(seat_here[:, :, None], seat_factors, 0.0), axis=1)
    lowrank_source = sum_mp(lowrank_source).astype(jnp.bfloat16)
    choice_mask_table = membership.astype(jnp.bfloat16)
    broadened_lines = (choice_mask_table[:, :, None] * lowrank_source[:, None, :]).reshape(
        prompt_ordinal, SHARD_PROMPTS * LOW_DIMENSION
    )
    raised_result_lines = projected_lowrank_right[request_ids].reshape(
        SHARD_PROMPTS * LOW_DIMENSION, 3 * channel_window * CHANNEL_LENGTH
    )
    adapter_query_key_value = jnp.dot(
        broadened_lines, raised_result_lines, preferred_element_type=jnp.float32
    ).reshape(prompt_ordinal, 3, channel_window, CHANNEL_LENGTH)
    token_positions = positions_of(segments)
    rotary_queries = apply_rotary(
        query_rows + adapter_query_key_value[:, 0], token_positions
    ).astype(jnp.bfloat16)
    rotary_keys = apply_rotary(
        key_value_rows[:, 0] + adapter_query_key_value[:, 1], token_positions
    ).astype(jnp.bfloat16)
    fresh_values = (key_value_rows[:, 1] + adapter_query_key_value[:, 2]).astype(jnp.bfloat16)
    kv_new = jnp.stack([rotary_keys, fresh_values], axis=1)
    own_pages = lax.dynamic_index_in_dim(request_pages, dp_index, 0, keepdims=False).reshape(
        SHARD_PROMPTS * PPR
    )
    whole_pool = lax.all_gather(key_value_cache, DP_AXES, axis=0, tiled=True)
    chosen = whole_pool[own_pages]
    keys_pre = jnp.transpose(chosen[:, 0], (1, 0, 2, 3)).reshape(
        channel_window, SHARD_PROMPTS * PPR * PAGE, CHANNEL_LENGTH
    )
    values_pre = jnp.transpose(chosen[:, 1], (1, 0, 2, 3)).reshape(
        channel_window, SHARD_PROMPTS * PPR * PAGE, CHANNEL_LENGTH
    )
    attended = attend_local(
        rotary_queries, rotary_keys, fresh_values, keys_pre, values_pre, segments
    )
    request_output_down = result_lowrank_left[request_ids]
    request_output_factors = jnp.einsum(
        "tc,rck->trk", attended, request_output_down, preferred_element_type=jnp.float32
    )
    output_adapter_piece = jnp.sum(
        jnp.where(membership[:, :, None], request_output_factors, 0.0), axis=1
    )
    result_lowrank_source = sum_mp(output_adapter_piece).astype(jnp.bfloat16)
    result_seat_lines = result_lowrank_right.shape[0]
    output_slots = mp_index * result_seat_lines + jnp.arange(result_seat_lines, dtype=jnp.int32)
    resident_here = (token_adapter_slot[:, None] == output_slots[None, :]).astype(jnp.bfloat16)
    broadened_result = (resident_here[:, :, None] * result_lowrank_source[:, None, :]).reshape(
        prompt_ordinal, result_seat_lines * LOW_DIMENSION
    )
    raised_window = result_lowrank_right.reshape(result_seat_lines * LOW_DIMENSION, HIDDEN_BREADTH)
    attn_sum = scatter_mp(
        (
            jnp.dot(attended, output_weight, preferred_element_type=jnp.float32)
            + jnp.dot(broadened_result, raised_window, preferred_element_type=jnp.float32)
        ).astype(jnp.bfloat16)
    ).astype(jnp.float32)
    after_attn = (residual + rms_scale(attn_sum, after_attention_gain)).astype(jnp.bfloat16)
    normed_ffw = rms_scale(after_attn.astype(jnp.float32), before_feedforward_gain).astype(
        jnp.bfloat16
    )
    piece = gather_mp(normed_ffw)
    gated = jnp.dot(piece, gate_matrix, preferred_element_type=jnp.float32)
    upward = jnp.dot(piece, up_matrix, preferred_element_type=jnp.float32)
    hidden = (jax.nn.gelu(gated, approximate=True) * upward).astype(jnp.bfloat16)
    ffw_sum = scatter_mp(
        jnp.dot(hidden, down_matrix, preferred_element_type=jnp.float32).astype(jnp.bfloat16)
    ).astype(jnp.float32)
    hidden_out = (
        after_attn.astype(jnp.float32) + rms_scale(ffw_sum, after_feedforward_gain)
    ).astype(jnp.bfloat16)
    return (hidden_out, kv_new)


def solution(mesh):
    fine_mesh = jax.sharding.Mesh(
        mesh.devices.reshape(2, 2, 4, 4, 2), DP_AXES + MP_AXES
    )
    return jax.shard_map(
        shards,
        mesh=fine_mesh,
        in_specs=(
            P(DP_AXES + MP_AXES, None),
            P(),
            P(),
            P(),
            P(),
            P(None, MP_AXES),
            P(None, None, MP_AXES, None),
            P(MP_AXES, None),
            P(None, MP_AXES),
            P(None, MP_AXES),
            P(MP_AXES, None),
            P(DP_AXES, None, MP_AXES, None, None),
            P(MP_AXES, None, None),
            P(None, None, None, MP_AXES, None),
            P(None, MP_AXES, None),
            P(MP_AXES, None, None),
            P(DP_AXES, None),
            P(DP_AXES, None),
            P(),
            P(),
        ),
        out_specs=(P(DP_AXES + MP_AXES, None), P(DP_AXES, None, MP_AXES, None)),
        check_vma=False,
    )
```

```python
import math

import jax
import jax.numpy as jnp
from jax import lax
from jax.sharding import PartitionSpec as P

HIDDEN_BREADTH = 4608
ASKING_CHANNELS = 32
CHANNEL_LENGTH = 128
NUM_LOW_TERMS = 64
LOW_DIMENSION = 16
SHARD_PROMPTS = 8
PPR = 4
PAGE = 16


EPS = 1e-06
SOFTCAP = 50.0

DP_AXES = ("zh", "c")
MP_AXES = ("x", "y", "zl")


AXIS_SIZES = {"zh": 2, "c": 2, "x": 4, "y": 4, "zl": 2}
PAIR_SWAP = ((0, 1), (1, 0))


PLANE_FLOWS = (("x", 1), ("x", -1), ("y", 1), ("y", -1))


def ring_gather(block, name, direction):
    size = AXIS_SIZES[name]
    me = lax.axis_index(name)
    perm = [(i, (i + direction) % size) for i in range(size)]
    gathered = jnp.zeros((size,) + block.shape, block.dtype)
    gathered = lax.dynamic_update_index_in_dim(gathered, block, me, 0)
    moving = block
    for step in range(size - 1):
        moving = lax.ppermute(moving, name, perm=perm)
        source = jnp.remainder(me - direction * (step + 1), size)
        gathered = lax.dynamic_update_index_in_dim(gathered, moving, source, 0)
    return gathered


def ring_scatter(blocks, name, direction):
    size = AXIS_SIZES[name]
    me = lax.axis_index(name)
    perm = [(i, (i + direction) % size) for i in range(size)]

    def own(offset):
        index = jnp.remainder(me + offset, size)
        return lax.dynamic_index_in_dim(blocks, index, 0, keepdims=False).astype(jnp.float32)

    moving = own(-direction).astype(blocks.dtype)
    for step in range(size - 1):
        arrived = lax.ppermute(moving, name, perm=perm).astype(jnp.float32)
        if step < size - 2:
            moving = (arrived + own(-direction * (step + 2))).astype(blocks.dtype)
    return arrived + own(0)


def gather_plane(values):
    quarter = values.shape[-1] // len(PLANE_FLOWS)
    pieces = []
    for index, (first, direction) in enumerate(PLANE_FLOWS):
        part = values[:, index * quarter:(index + 1) * quarter]
        if first == "x":
            part = ring_gather(ring_gather(part, "y", direction), "x", direction)
        else:
            part = jnp.swapaxes(ring_gather(ring_gather(part, "x", direction), "y", direction), 0, 1)
        pieces.append(part.reshape(-1, quarter))
    return jnp.concatenate(pieces, axis=-1)


def scatter_plane(values):
    quarter = values.shape[-1] // len(PLANE_FLOWS)
    rows = values.reshape(AXIS_SIZES["x"], AXIS_SIZES["y"], -1, values.shape[-1])
    pieces = []
    for index, (first, direction) in enumerate(PLANE_FLOWS):
        part = rows[..., index * quarter:(index + 1) * quarter]
        if first == "x":
            part = ring_scatter(part, "x", direction).astype(values.dtype)
            part = ring_scatter(part, "y", direction)
        else:
            part = ring_scatter(jnp.swapaxes(part, 0, 1), "y", direction).astype(values.dtype)
            part = ring_scatter(part, "x", direction)
        pieces.append(part)
    return jnp.concatenate(pieces, axis=-1)


def gather_mp(values):
    other = lax.ppermute(values, "zl", perm=PAIR_SWAP)
    lead = lax.axis_index("zl") == 0
    values = jnp.concatenate(
        [jnp.where(lead, values, other), jnp.where(lead, other, values)], axis=0
    )
    return gather_plane(values)


def scatter_mp(values):
    group = AXIS_SIZES["x"] * AXIS_SIZES["y"] * AXIS_SIZES["zl"]
    values = lax.all_to_all(values, MP_AXES, 0, 0, tiled=True)
    return jnp.sum(values.reshape(group, -1, values.shape[-1]).astype(jnp.float32), axis=0)


def sum_mp(values):
    for name in ("zl", "y", "x"):
        step = 1
        while step < AXIS_SIZES[name]:
            partner = [(i, i ^ step) for i in range(AXIS_SIZES[name])]
            values = values + lax.ppermute(values, name, perm=partner)
            step *= 2
    return values


def rms_scale(values, scaling):
    mean_square = jnp.mean(values * values, axis=-1, keepdims=True)
    return values * lax.rsqrt(mean_square + EPS) * scaling


def apply_rotary(values, token_positions):
    half_dim = values.shape[-1] // 2
    frequency = 10000.0 ** (-2.0 * jnp.arange(half_dim, dtype=jnp.float32) / values.shape[-1])
    angles = token_positions.astype(jnp.float32)[:, None] * frequency[None, :]
    cosine = jnp.cos(angles)[:, None, :]
    sine_part = jnp.sin(angles)[:, None, :]
    first_half = values[..., :half_dim]
    second_half = values[..., half_dim:]
    return jnp.concatenate(
        [
            first_half * cosine - second_half * sine_part,
            second_half * cosine + first_half * sine_part,
        ],
        axis=-1,
    )


def positions_of(segments):
    length = segments.shape[0]
    earlier = jnp.sum((segments[None, :] < segments[:, None]).astype(jnp.int32), axis=1)
    return PPR * PAGE + jnp.arange(length, dtype=jnp.int32) - earlier


def capped(scores):
    return SOFTCAP * jnp.tanh(scores / SOFTCAP)


def attend_local(query_rows, keys_new, fresh_values, keys_pre, values_pre, segments):
    scale_factor = 1.0 / math.sqrt(HIDDEN_BREADTH // ASKING_CHANNELS)
    length = segments.shape[0]
    prefix_owner = jnp.arange(keys_pre.shape[1], dtype=jnp.int32) // (PPR * PAGE)
    mask_pre = (prefix_owner[None, :] == segments[:, None])[None]
    ordinal = jnp.arange(length, dtype=jnp.int32)
    mask_new = ((segments[None, :] == segments[:, None]) & (ordinal[None, :] <= ordinal[:, None]))[
        None
    ]
    scores_pre = (
        jnp.einsum("thd,hjd->htj", query_rows, keys_pre, preferred_element_type=jnp.float32)
        * scale_factor
    )
    scores_new = (
        jnp.einsum("thd,uhd->htu", query_rows, keys_new, preferred_element_type=jnp.float32)
        * scale_factor
    )
    weight_pre = jnp.where(mask_pre, jnp.exp(capped(scores_pre)), 0.0)
    weight_new = jnp.where(mask_new, jnp.exp(capped(scores_new)), 0.0)
    totals = jnp.sum(weight_pre, axis=-1, keepdims=True) + jnp.sum(
        weight_new, axis=-1, keepdims=True
    )
    probs_pre = (weight_pre / totals).astype(jnp.bfloat16)
    probs_new = (weight_new / totals).astype(jnp.bfloat16)
    mixture = jnp.einsum("htj,hjd->thd", probs_pre, values_pre, preferred_element_type=jnp.float32)
    mixture = mixture + jnp.einsum(
        "htu,uhd->thd", probs_new, fresh_values, preferred_element_type=jnp.float32
    )
    return mixture.astype(jnp.bfloat16).reshape(length, -1)


def shards(
    residual_input,
    before_attention_gain,
    after_attention_gain,
    before_feedforward_gain,
    after_feedforward_gain,
    query_weight,
    key_value_weight,
    output_weight,
    gate_matrix,
    up_matrix,
    down_matrix,
    key_value_cache,
    projected_lowrank_left,
    projected_lowrank_right,
    result_lowrank_left,
    result_lowrank_right,
    token_request,
    lowrank_choice_by_prompt,
    adapter_position,
    request_pages,
):
    mp_index = lax.axis_index(MP_AXES)
    dp_index = lax.axis_index(DP_AXES)
    residual = residual_input.astype(jnp.float32)
    normed_rows = rms_scale(residual, before_attention_gain).astype(jnp.bfloat16)
    normalized_rows = gather_mp(normed_rows)
    prompt_ordinal = normalized_rows.shape[0]
    channel_window = query_weight.shape[1] // CHANNEL_LENGTH
    query_rows = jnp.dot(normalized_rows, query_weight, preferred_element_type=jnp.float32).reshape(
        prompt_ordinal, channel_window, CHANNEL_LENGTH
    )
    key_value_rows = jnp.dot(
        normalized_rows,
        key_value_weight.reshape(HIDDEN_BREADTH, 2 * channel_window * CHANNEL_LENGTH),
        preferred_element_type=jnp.float32,
    ).reshape(prompt_ordinal, 2, channel_window, CHANNEL_LENGTH)
    segments = token_request[0]
    request_ids = lowrank_choice_by_prompt[0]
    request_range = jnp.arange(SHARD_PROMPTS, dtype=jnp.int32)
    membership = segments[:, None] == request_range[None, :]
    adapter_range = jnp.arange(NUM_LOW_TERMS, dtype=jnp.int32)
    token_adapter = jnp.sum(jnp.where(membership, request_ids[None, :], 0), axis=1)
    token_adapter_slot = jnp.sum(
        jnp.where(token_adapter[:, None] == adapter_range[None, :], adapter_position[None, :], 0),
        axis=1,
    )
    seat_count = projected_lowrank_left.shape[0]
    local_seats = mp_index * seat_count + jnp.arange(seat_count, dtype=jnp.int32)
    seat_factors = jnp.einsum(
        "td,sdk->tsk", normalized_rows, projected_lowrank_left, preferred_element_type=jnp.float32
    )
    seat_here = token_adapter_slot[:, None] == local_seats[None, :]
    lowrank_source = jnp.sum(jnp.where(seat_here[:, :, None], seat_factors, 0.0), axis=1)
    lowrank_source = sum_mp(lowrank_source).astype(jnp.bfloat16)
    choice_mask_table = membership.astype(jnp.bfloat16)
    broadened_lines = (choice_mask_table[:, :, None] * lowrank_source[:, None, :]).reshape(
        prompt_ordinal, SHARD_PROMPTS * LOW_DIMENSION
    )
    raised_result_lines = projected_lowrank_right[request_ids].reshape(
        SHARD_PROMPTS * LOW_DIMENSION, 3 * channel_window * CHANNEL_LENGTH
    )
    adapter_query_key_value = jnp.dot(
        broadened_lines, raised_result_lines, preferred_element_type=jnp.float32
    ).reshape(prompt_ordinal, 3, channel_window, CHANNEL_LENGTH)
    token_positions = positions_of(segments)
    rotary_queries = apply_rotary(
        query_rows + adapter_query_key_value[:, 0], token_positions
    ).astype(jnp.bfloat16)
    rotary_keys = apply_rotary(
        key_value_rows[:, 0] + adapter_query_key_value[:, 1], token_positions
    ).astype(jnp.bfloat16)
    fresh_values = (key_value_rows[:, 1] + adapter_query_key_value[:, 2]).astype(jnp.bfloat16)
    kv_new = jnp.stack([rotary_keys, fresh_values], axis=1)
    own_pages = lax.dynamic_index_in_dim(request_pages, dp_index, 0, keepdims=False).reshape(
        SHARD_PROMPTS * PPR
    )
    whole_pool = lax.all_gather(key_value_cache, DP_AXES, axis=0, tiled=True)
    chosen = whole_pool[own_pages]
    keys_pre = jnp.transpose(chosen[:, 0], (1, 0, 2, 3)).reshape(
        channel_window, SHARD_PROMPTS * PPR * PAGE, CHANNEL_LENGTH
    )
    values_pre = jnp.transpose(chosen[:, 1], (1, 0, 2, 3)).reshape(
        channel_window, SHARD_PROMPTS * PPR * PAGE, CHANNEL_LENGTH
    )
    attended = attend_local(
        rotary_queries, rotary_keys, fresh_values, keys_pre, values_pre, segments
    )
    request_output_down = result_lowrank_left[request_ids]
    request_output_factors = jnp.einsum(
        "tc,rck->trk", attended, request_output_down, preferred_element_type=jnp.float32
    )
    output_adapter_piece = jnp.sum(
        jnp.where(membership[:, :, None], request_output_factors, 0.0), axis=1
    )
    result_lowrank_source = sum_mp(output_adapter_piece).astype(jnp.bfloat16)
    result_seat_lines = result_lowrank_right.shape[0]
    output_slots = mp_index * result_seat_lines + jnp.arange(result_seat_lines, dtype=jnp.int32)
    resident_here = (token_adapter_slot[:, None] == output_slots[None, :]).astype(jnp.bfloat16)
    broadened_result = (resident_here[:, :, None] * result_lowrank_source[:, None, :]).reshape(
        prompt_ordinal, result_seat_lines * LOW_DIMENSION
    )
    raised_window = result_lowrank_right.reshape(result_seat_lines * LOW_DIMENSION, HIDDEN_BREADTH)
    attn_sum = scatter_mp(
        (
            jnp.dot(attended, output_weight, preferred_element_type=jnp.float32)
            + jnp.dot(broadened_result, raised_window, preferred_element_type=jnp.float32)
        ).astype(jnp.bfloat16)
    ).astype(jnp.float32)
    after_attn = (residual + rms_scale(attn_sum, after_attention_gain)).astype(jnp.bfloat16)
    normed_ffw = rms_scale(after_attn.astype(jnp.float32), before_feedforward_gain).astype(
        jnp.bfloat16
    )
    piece = gather_mp(normed_ffw)
    gated = jnp.dot(piece, gate_matrix, preferred_element_type=jnp.float32)
    upward = jnp.dot(piece, up_matrix, preferred_element_type=jnp.float32)
    hidden = (jax.nn.gelu(gated, approximate=True) * upward).astype(jnp.bfloat16)
    ffw_sum = scatter_mp(
        jnp.dot(hidden, down_matrix, preferred_element_type=jnp.float32).astype(jnp.bfloat16)
    ).astype(jnp.float32)
    hidden_out = (
        after_attn.astype(jnp.float32) + rms_scale(ffw_sum, after_feedforward_gain)
    ).astype(jnp.bfloat16)
    return (hidden_out, kv_new)


def solution(mesh):
    fine_mesh = jax.sharding.Mesh(
        mesh.devices.reshape(2, 2, 4, 4, 2), DP_AXES + MP_AXES
    )
    return jax.shard_map(
        shards,
        mesh=fine_mesh,
        in_specs=(
            P(DP_AXES + MP_AXES, None),
            P(),
            P(),
            P(),
            P(),
            P(None, MP_AXES),
            P(None, None, MP_AXES, None),
            P(MP_AXES, None),
            P(None, MP_AXES),
            P(None, MP_AXES),
            P(MP_AXES, None),
            P(DP_AXES, None, MP_AXES, None, None),
            P(MP_AXES, None, None),
            P(None, None, None, MP_AXES, None),
            P(None, MP_AXES, None),
            P(MP_AXES, None, None),
            P(DP_AXES, None),
            P(DP_AXES, None),
            P(),
            P(),
        ),
        out_specs=(P(DP_AXES + MP_AXES, None), P(DP_AXES, None, MP_AXES, None)),
        check_vma=False,
    )
```

```python
import math

import jax
import jax.numpy as jnp
from jax import lax
from jax.sharding import PartitionSpec as P

HIDDEN_BREADTH = 4608
ASKING_CHANNELS = 32
CHANNEL_LENGTH = 128
NUM_LOW_TERMS = 64
LOW_DIMENSION = 16
SHARD_PROMPTS = 8
PPR = 4
PAGE = 16


EPS = 1e-06
SOFTCAP = 50.0

DP_AXES = ("zh", "c")
MP_AXES = ("x", "y", "zl")


AXIS_SIZES = {"zh": 2, "c": 2, "x": 4, "y": 4, "zl": 2}
PAIR_SWAP = ((0, 1), (1, 0))


PLANE_FLOWS = (("x", 1), ("x", -1), ("y", 1), ("y", -1))


def ring_gather(block, name, direction):
    size = AXIS_SIZES[name]
    me = lax.axis_index(name)
    perm = [(i, (i + direction) % size) for i in range(size)]
    gathered = jnp.zeros((size,) + block.shape, block.dtype)
    gathered = lax.dynamic_update_index_in_dim(gathered, block, me, 0)
    moving = block
    for step in range(size - 1):
        moving = lax.ppermute(moving, name, perm=perm)
        source = jnp.remainder(me - direction * (step + 1), size)
        gathered = lax.dynamic_update_index_in_dim(gathered, moving, source, 0)
    return gathered


def ring_scatter(blocks, name, direction):
    size = AXIS_SIZES[name]
    me = lax.axis_index(name)
    perm = [(i, (i + direction) % size) for i in range(size)]

    def own(offset):
        index = jnp.remainder(me + offset, size)
        return lax.dynamic_index_in_dim(blocks, index, 0, keepdims=False).astype(jnp.float32)

    moving = own(-direction).astype(blocks.dtype)
    for step in range(size - 1):
        arrived = lax.ppermute(moving, name, perm=perm).astype(jnp.float32)
        if step < size - 2:
            moving = (arrived + own(-direction * (step + 2))).astype(blocks.dtype)
    return arrived + own(0)


def gather_plane(values):
    quarter = values.shape[-1] // len(PLANE_FLOWS)
    pieces = []
    for index, (first, direction) in enumerate(PLANE_FLOWS):
        part = values[:, index * quarter:(index + 1) * quarter]
        if first == "x":
            part = ring_gather(ring_gather(part, "y", direction), "x", direction)
        else:
            part = jnp.swapaxes(ring_gather(ring_gather(part, "x", direction), "y", direction), 0, 1)
        pieces.append(part.reshape(-1, quarter))
    return jnp.concatenate(pieces, axis=-1)


def scatter_plane(values):
    quarter = values.shape[-1] // len(PLANE_FLOWS)
    rows = values.reshape(AXIS_SIZES["x"], AXIS_SIZES["y"], -1, values.shape[-1])
    pieces = []
    for index, (first, direction) in enumerate(PLANE_FLOWS):
        part = rows[..., index * quarter:(index + 1) * quarter]
        if first == "x":
            part = ring_scatter(part, "x", direction).astype(values.dtype)
            part = ring_scatter(part, "y", direction)
        else:
            part = ring_scatter(jnp.swapaxes(part, 0, 1), "y", direction).astype(values.dtype)
            part = ring_scatter(part, "x", direction)
        pieces.append(part)
    return jnp.concatenate(pieces, axis=-1)


def gather_mp(values):
    other = lax.ppermute(values, "zl", perm=PAIR_SWAP)
    lead = lax.axis_index("zl") == 0
    values = jnp.concatenate(
        [jnp.where(lead, values, other), jnp.where(lead, other, values)], axis=0
    )
    return gather_plane(values)


def scatter_mp(values):
    plane = AXIS_SIZES["x"] * AXIS_SIZES["y"]
    values = lax.all_to_all(values, ("x", "y"), 0, 0, tiled=True)
    values = jnp.sum(
        values.reshape(plane, -1, values.shape[-1]).astype(jnp.float32), axis=0
    )
    half = values.shape[0] // 2
    lead = lax.axis_index("zl") == 0
    keep = jnp.where(lead, values[:half], values[half:])
    send = jnp.where(lead, values[half:], values[:half]).astype(jnp.bfloat16)
    other = lax.ppermute(send, "zl", perm=PAIR_SWAP)
    return keep + other.astype(jnp.float32)


def sum_mp(values):
    group = AXIS_SIZES["x"] * AXIS_SIZES["y"] * AXIS_SIZES["zl"]
    copies = jnp.broadcast_to(values[None], (group,) + values.shape)
    return jnp.sum(lax.all_to_all(copies, MP_AXES, 0, 0, tiled=True), axis=0)


def rms_scale(values, scaling):
    mean_square = jnp.mean(values * values, axis=-1, keepdims=True)
    return values * lax.rsqrt(mean_square + EPS) * scaling


def apply_rotary(values, token_positions):
    half_dim = values.shape[-1] // 2
    frequency = 10000.0 ** (-2.0 * jnp.arange(half_dim, dtype=jnp.float32) / values.shape[-1])
    angles = token_positions.astype(jnp.float32)[:, None] * frequency[None, :]
    cosine = jnp.cos(angles)[:, None, :]
    sine_part = jnp.sin(angles)[:, None, :]
    first_half = values[..., :half_dim]
    second_half = values[..., half_dim:]
    return jnp.concatenate(
        [
            first_half * cosine - second_half * sine_part,
            second_half * cosine + first_half * sine_part,
        ],
        axis=-1,
    )


def positions_of(segments):
    length = segments.shape[0]
    earlier = jnp.sum((segments[None, :] < segments[:, None]).astype(jnp.int32), axis=1)
    return PPR * PAGE + jnp.arange(length, dtype=jnp.int32) - earlier


def capped(scores):
    return SOFTCAP * jnp.tanh(scores / SOFTCAP)


def attend_local(query_rows, keys_new, fresh_values, keys_pre, values_pre, segments):
    scale_factor = 1.0 / math.sqrt(HIDDEN_BREADTH // ASKING_CHANNELS)
    length = segments.shape[0]
    prefix_owner = jnp.arange(keys_pre.shape[1], dtype=jnp.int32) // (PPR * PAGE)
    mask_pre = (prefix_owner[None, :] == segments[:, None])[None]
    ordinal = jnp.arange(length, dtype=jnp.int32)
    mask_new = ((segments[None, :] == segments[:, None]) & (ordinal[None, :] <= ordinal[:, None]))[
        None
    ]
    scores_pre = (
        jnp.einsum("thd,hjd->htj", query_rows, keys_pre, preferred_element_type=jnp.float32)
        * scale_factor
    )
    scores_new = (
        jnp.einsum("thd,uhd->htu", query_rows, keys_new, preferred_element_type=jnp.float32)
        * scale_factor
    )
    weight_pre = jnp.where(mask_pre, jnp.exp(capped(scores_pre)), 0.0)
    weight_new = jnp.where(mask_new, jnp.exp(capped(scores_new)), 0.0)
    totals = jnp.sum(weight_pre, axis=-1, keepdims=True) + jnp.sum(
        weight_new, axis=-1, keepdims=True
    )
    probs_pre = (weight_pre / totals).astype(jnp.bfloat16)
    probs_new = (weight_new / totals).astype(jnp.bfloat16)
    mixture = jnp.einsum("htj,hjd->thd", probs_pre, values_pre, preferred_element_type=jnp.float32)
    mixture = mixture + jnp.einsum(
        "htu,uhd->thd", probs_new, fresh_values, preferred_element_type=jnp.float32
    )
    return mixture.astype(jnp.bfloat16).reshape(length, -1)


def shards(
    residual_input,
    before_attention_gain,
    after_attention_gain,
    before_feedforward_gain,
    after_feedforward_gain,
    query_weight,
    key_value_weight,
    output_weight,
    gate_matrix,
    up_matrix,
    down_matrix,
    key_value_cache,
    projected_lowrank_left,
    projected_lowrank_right,
    result_lowrank_left,
    result_lowrank_right,
    token_request,
    lowrank_choice_by_prompt,
    adapter_position,
    request_pages,
):
    mp_index = lax.axis_index(MP_AXES)
    dp_index = lax.axis_index(DP_AXES)
    residual = residual_input.astype(jnp.float32)
    normed_rows = rms_scale(residual, before_attention_gain).astype(jnp.bfloat16)
    normalized_rows = gather_mp(normed_rows)
    prompt_ordinal = normalized_rows.shape[0]
    channel_window = query_weight.shape[1] // CHANNEL_LENGTH
    query_rows = jnp.dot(normalized_rows, query_weight, preferred_element_type=jnp.float32).reshape(
        prompt_ordinal, channel_window, CHANNEL_LENGTH
    )
    key_value_rows = jnp.dot(
        normalized_rows,
        key_value_weight.reshape(HIDDEN_BREADTH, 2 * channel_window * CHANNEL_LENGTH),
        preferred_element_type=jnp.float32,
    ).reshape(prompt_ordinal, 2, channel_window, CHANNEL_LENGTH)
    segments = token_request[0]
    request_ids = lowrank_choice_by_prompt[0]
    request_range = jnp.arange(SHARD_PROMPTS, dtype=jnp.int32)
    membership = segments[:, None] == request_range[None, :]
    adapter_range = jnp.arange(NUM_LOW_TERMS, dtype=jnp.int32)
    token_adapter = jnp.sum(jnp.where(membership, request_ids[None, :], 0), axis=1)
    token_adapter_slot = jnp.sum(
        jnp.where(token_adapter[:, None] == adapter_range[None, :], adapter_position[None, :], 0),
        axis=1,
    )
    seat_count = projected_lowrank_left.shape[0]
    local_seats = mp_index * seat_count + jnp.arange(seat_count, dtype=jnp.int32)
    seat_factors = jnp.einsum(
        "td,sdk->tsk", normalized_rows, projected_lowrank_left, preferred_element_type=jnp.float32
    )
    seat_here = token_adapter_slot[:, None] == local_seats[None, :]
    lowrank_source = jnp.sum(jnp.where(seat_here[:, :, None], seat_factors, 0.0), axis=1)
    lowrank_source = sum_mp(lowrank_source).astype(jnp.bfloat16)
    choice_mask_table = membership.astype(jnp.bfloat16)
    broadened_lines = (choice_mask_table[:, :, None] * lowrank_source[:, None, :]).reshape(
        prompt_ordinal, SHARD_PROMPTS * LOW_DIMENSION
    )
    raised_result_lines = projected_lowrank_right[request_ids].reshape(
        SHARD_PROMPTS * LOW_DIMENSION, 3 * channel_window * CHANNEL_LENGTH
    )
    adapter_query_key_value = jnp.dot(
        broadened_lines, raised_result_lines, preferred_element_type=jnp.float32
    ).reshape(prompt_ordinal, 3, channel_window, CHANNEL_LENGTH)
    token_positions = positions_of(segments)
    rotary_queries = apply_rotary(
        query_rows + adapter_query_key_value[:, 0], token_positions
    ).astype(jnp.bfloat16)
    rotary_keys = apply_rotary(
        key_value_rows[:, 0] + adapter_query_key_value[:, 1], token_positions
    ).astype(jnp.bfloat16)
    fresh_values = (key_value_rows[:, 1] + adapter_query_key_value[:, 2]).astype(jnp.bfloat16)
    kv_new = jnp.stack([rotary_keys, fresh_values], axis=1)
    own_pages = lax.dynamic_index_in_dim(request_pages, dp_index, 0, keepdims=False).reshape(
        SHARD_PROMPTS * PPR
    )
    whole_pool = lax.all_gather(key_value_cache, DP_AXES, axis=0, tiled=True)
    chosen = whole_pool[own_pages]
    keys_pre = jnp.transpose(chosen[:, 0], (1, 0, 2, 3)).reshape(
        channel_window, SHARD_PROMPTS * PPR * PAGE, CHANNEL_LENGTH
    )
    values_pre = jnp.transpose(chosen[:, 1], (1, 0, 2, 3)).reshape(
        channel_window, SHARD_PROMPTS * PPR * PAGE, CHANNEL_LENGTH
    )
    attended = attend_local(
        rotary_queries, rotary_keys, fresh_values, keys_pre, values_pre, segments
    )
    request_output_down = result_lowrank_left[request_ids]
    request_output_factors = jnp.einsum(
        "tc,rck->trk", attended, request_output_down, preferred_element_type=jnp.float32
    )
    output_adapter_piece = jnp.sum(
        jnp.where(membership[:, :, None], request_output_factors, 0.0), axis=1
    )
    result_lowrank_source = sum_mp(output_adapter_piece).astype(jnp.bfloat16)
    result_seat_lines = result_lowrank_right.shape[0]
    output_slots = mp_index * result_seat_lines + jnp.arange(result_seat_lines, dtype=jnp.int32)
    resident_here = (token_adapter_slot[:, None] == output_slots[None, :]).astype(jnp.bfloat16)
    broadened_result = (resident_here[:, :, None] * result_lowrank_source[:, None, :]).reshape(
        prompt_ordinal, result_seat_lines * LOW_DIMENSION
    )
    raised_window = result_lowrank_right.reshape(result_seat_lines * LOW_DIMENSION, HIDDEN_BREADTH)
    attn_sum = scatter_mp(
        (
            jnp.dot(attended, output_weight, preferred_element_type=jnp.float32)
            + jnp.dot(broadened_result, raised_window, preferred_element_type=jnp.float32)
        ).astype(jnp.bfloat16)
    ).astype(jnp.float32)
    after_attn = (residual + rms_scale(attn_sum, after_attention_gain)).astype(jnp.bfloat16)
    normed_ffw = rms_scale(after_attn.astype(jnp.float32), before_feedforward_gain).astype(
        jnp.bfloat16
    )
    piece = gather_mp(normed_ffw)
    gated = jnp.dot(piece, gate_matrix, preferred_element_type=jnp.float32)
    upward = jnp.dot(piece, up_matrix, preferred_element_type=jnp.float32)
    hidden = (jax.nn.gelu(gated, approximate=True) * upward).astype(jnp.bfloat16)
    ffw_sum = scatter_mp(
        jnp.dot(hidden, down_matrix, preferred_element_type=jnp.float32).astype(jnp.bfloat16)
    ).astype(jnp.float32)
    hidden_out = (
        after_attn.astype(jnp.float32) + rms_scale(ffw_sum, after_feedforward_gain)
    ).astype(jnp.bfloat16)
    return (hidden_out, kv_new)


def solution(mesh):
    fine_mesh = jax.sharding.Mesh(
        mesh.devices.reshape(2, 2, 4, 4, 2), DP_AXES + MP_AXES
    )
    return jax.shard_map(
        shards,
        mesh=fine_mesh,
        in_specs=(
            P(DP_AXES + MP_AXES, None),
            P(),
            P(),
            P(),
            P(),
            P(None, MP_AXES),
            P(None, None, MP_AXES, None),
            P(MP_AXES, None),
            P(None, MP_AXES),
            P(None, MP_AXES),
            P(MP_AXES, None),
            P(DP_AXES, None, MP_AXES, None, None),
            P(MP_AXES, None, None),
            P(None, None, None, MP_AXES, None),
            P(None, MP_AXES, None),
            P(MP_AXES, None, None),
            P(DP_AXES, None),
            P(DP_AXES, None),
            P(),
            P(),
        ),
        out_specs=(P(DP_AXES + MP_AXES, None), P(DP_AXES, None, MP_AXES, None)),
        check_vma=False,
    )
```

```python
import math

import jax
import jax.numpy as jnp
from jax import lax
from jax.sharding import PartitionSpec as P

HIDDEN_BREADTH = 4608
ASKING_CHANNELS = 32
CHANNEL_LENGTH = 128
NUM_LOW_TERMS = 64
LOW_DIMENSION = 16
SHARD_PROMPTS = 8
PPR = 4
PAGE = 16


EPS = 1e-06
SOFTCAP = 50.0

DP_AXES = ("zh", "c")
MP_AXES = ("x", "y", "zl")


AXIS_SIZES = {"zh": 2, "c": 2, "x": 4, "y": 4, "zl": 2}
PAIR_SWAP = ((0, 1), (1, 0))


PLANE_FLOWS = (("x", 1), ("x", -1), ("y", 1), ("y", -1))


def ring_gather(block, name, direction):
    size = AXIS_SIZES[name]
    me = lax.axis_index(name)
    perm = [(i, (i + direction) % size) for i in range(size)]
    gathered = jnp.zeros((size,) + block.shape, block.dtype)
    gathered = lax.dynamic_update_index_in_dim(gathered, block, me, 0)
    moving = block
    for step in range(size - 1):
        moving = lax.ppermute(moving, name, perm=perm)
        source = jnp.remainder(me - direction * (step + 1), size)
        gathered = lax.dynamic_update_index_in_dim(gathered, moving, source, 0)
    return gathered


def ring_scatter(blocks, name, direction):
    size = AXIS_SIZES[name]
    me = lax.axis_index(name)
    perm = [(i, (i + direction) % size) for i in range(size)]

    def own(offset):
        index = jnp.remainder(me + offset, size)
        return lax.dynamic_index_in_dim(blocks, index, 0, keepdims=False).astype(jnp.float32)

    moving = own(-direction).astype(blocks.dtype)
    for step in range(size - 1):
        arrived = lax.ppermute(moving, name, perm=perm).astype(jnp.float32)
        if step < size - 2:
            moving = (arrived + own(-direction * (step + 2))).astype(blocks.dtype)
    return arrived + own(0)


def gather_plane(values):
    half = values.shape[-1] // 2
    quarter = half // 2
    pieces = []
    for index, (first, second) in enumerate((("y", "x"), ("x", "y"))):
        part = ring_gather(values[:, index * half:(index + 1) * half], first, 1)
        part = jnp.concatenate(
            [
                ring_gather(part[..., :quarter], second, 1),
                ring_gather(part[..., quarter:], second, -1),
            ],
            axis=-1,
        )
        if first == "x":
            part = jnp.swapaxes(part, 0, 1)
        pieces.append(part.reshape(-1, half))
    return jnp.concatenate(pieces, axis=-1)


def scatter_plane(values):
    quarter = values.shape[-1] // len(PLANE_FLOWS)
    rows = values.reshape(AXIS_SIZES["x"], AXIS_SIZES["y"], -1, values.shape[-1])
    pieces = []
    for index, (first, direction) in enumerate(PLANE_FLOWS):
        part = rows[..., index * quarter:(index + 1) * quarter]
        if first == "x":
            part = ring_scatter(part, "x", direction).astype(values.dtype)
            part = ring_scatter(part, "y", direction)
        else:
            part = ring_scatter(jnp.swapaxes(part, 0, 1), "y", direction).astype(values.dtype)
            part = ring_scatter(part, "x", direction)
        pieces.append(part)
    return jnp.concatenate(pieces, axis=-1)


def gather_mp(values):
    other = lax.ppermute(values, "zl", perm=PAIR_SWAP)
    lead = lax.axis_index("zl") == 0
    values = jnp.concatenate(
        [jnp.where(lead, values, other), jnp.where(lead, other, values)], axis=0
    )
    return gather_plane(values)


def scatter_mp(values):
    plane = AXIS_SIZES["x"] * AXIS_SIZES["y"]
    values = lax.all_to_all(values, ("x", "y"), 0, 0, tiled=True)
    values = jnp.sum(
        values.reshape(plane, -1, values.shape[-1]).astype(jnp.float32), axis=0
    )
    half = values.shape[0] // 2
    lead = lax.axis_index("zl") == 0
    keep = jnp.where(lead, values[:half], values[half:])
    send = jnp.where(lead, values[half:], values[:half]).astype(jnp.bfloat16)
    other = lax.ppermute(send, "zl", perm=PAIR_SWAP)
    return keep + other.astype(jnp.float32)


def sum_mp(values):
    for name in ("zl", "y", "x"):
        step = 1
        while step < AXIS_SIZES[name]:
            partner = [(i, i ^ step) for i in range(AXIS_SIZES[name])]
            values = values + lax.ppermute(values, name, perm=partner)
            step *= 2
    return values


def rms_scale(values, scaling):
    mean_square = jnp.mean(values * values, axis=-1, keepdims=True)
    return values * lax.rsqrt(mean_square + EPS) * scaling


def apply_rotary(values, token_positions):
    half_dim = values.shape[-1] // 2
    frequency = 10000.0 ** (-2.0 * jnp.arange(half_dim, dtype=jnp.float32) / values.shape[-1])
    angles = token_positions.astype(jnp.float32)[:, None] * frequency[None, :]
    cosine = jnp.cos(angles)[:, None, :]
    sine_part = jnp.sin(angles)[:, None, :]
    first_half = values[..., :half_dim]
    second_half = values[..., half_dim:]
    return jnp.concatenate(
        [
            first_half * cosine - second_half * sine_part,
            second_half * cosine + first_half * sine_part,
        ],
        axis=-1,
    )


def positions_of(segments):
    length = segments.shape[0]
    earlier = jnp.sum((segments[None, :] < segments[:, None]).astype(jnp.int32), axis=1)
    return PPR * PAGE + jnp.arange(length, dtype=jnp.int32) - earlier


def capped(scores):
    return SOFTCAP * jnp.tanh(scores / SOFTCAP)


def attend_local(query_rows, keys_new, fresh_values, keys_pre, values_pre, segments):
    scale_factor = 1.0 / math.sqrt(HIDDEN_BREADTH // ASKING_CHANNELS)
    length = segments.shape[0]
    prefix_owner = jnp.arange(keys_pre.shape[1], dtype=jnp.int32) // (PPR * PAGE)
    mask_pre = (prefix_owner[None, :] == segments[:, None])[None]
    ordinal = jnp.arange(length, dtype=jnp.int32)
    mask_new = ((segments[None, :] == segments[:, None]) & (ordinal[None, :] <= ordinal[:, None]))[
        None
    ]
    scores_pre = (
        jnp.einsum("thd,hjd->htj", query_rows, keys_pre, preferred_element_type=jnp.float32)
        * scale_factor
    )
    scores_new = (
        jnp.einsum("thd,uhd->htu", query_rows, keys_new, preferred_element_type=jnp.float32)
        * scale_factor
    )
    weight_pre = jnp.where(mask_pre, jnp.exp(capped(scores_pre)), 0.0)
    weight_new = jnp.where(mask_new, jnp.exp(capped(scores_new)), 0.0)
    totals = jnp.sum(weight_pre, axis=-1, keepdims=True) + jnp.sum(
        weight_new, axis=-1, keepdims=True
    )
    probs_pre = (weight_pre / totals).astype(jnp.bfloat16)
    probs_new = (weight_new / totals).astype(jnp.bfloat16)
    mixture = jnp.einsum("htj,hjd->thd", probs_pre, values_pre, preferred_element_type=jnp.float32)
    mixture = mixture + jnp.einsum(
        "htu,uhd->thd", probs_new, fresh_values, preferred_element_type=jnp.float32
    )
    return mixture.astype(jnp.bfloat16).reshape(length, -1)


def shards(
    residual_input,
    before_attention_gain,
    after_attention_gain,
    before_feedforward_gain,
    after_feedforward_gain,
    query_weight,
    key_value_weight,
    output_weight,
    gate_matrix,
    up_matrix,
    down_matrix,
    key_value_cache,
    projected_lowrank_left,
    projected_lowrank_right,
    result_lowrank_left,
    result_lowrank_right,
    token_request,
    lowrank_choice_by_prompt,
    adapter_position,
    request_pages,
):
    mp_index = lax.axis_index(MP_AXES)
    dp_index = lax.axis_index(DP_AXES)
    residual = residual_input.astype(jnp.float32)
    normed_rows = rms_scale(residual, before_attention_gain).astype(jnp.bfloat16)
    normalized_rows = gather_mp(normed_rows)
    prompt_ordinal = normalized_rows.shape[0]
    channel_window = query_weight.shape[1] // CHANNEL_LENGTH
    query_rows = jnp.dot(normalized_rows, query_weight, preferred_element_type=jnp.float32).reshape(
        prompt_ordinal, channel_window, CHANNEL_LENGTH
    )
    key_value_rows = jnp.dot(
        normalized_rows,
        key_value_weight.reshape(HIDDEN_BREADTH, 2 * channel_window * CHANNEL_LENGTH),
        preferred_element_type=jnp.float32,
    ).reshape(prompt_ordinal, 2, channel_window, CHANNEL_LENGTH)
    segments = token_request[0]
    request_ids = lowrank_choice_by_prompt[0]
    request_range = jnp.arange(SHARD_PROMPTS, dtype=jnp.int32)
    membership = segments[:, None] == request_range[None, :]
    adapter_range = jnp.arange(NUM_LOW_TERMS, dtype=jnp.int32)
    token_adapter = jnp.sum(jnp.where(membership, request_ids[None, :], 0), axis=1)
    token_adapter_slot = jnp.sum(
        jnp.where(token_adapter[:, None] == adapter_range[None, :], adapter_position[None, :], 0),
        axis=1,
    )
    seat_count = projected_lowrank_left.shape[0]
    local_seats = mp_index * seat_count + jnp.arange(seat_count, dtype=jnp.int32)
    seat_factors = jnp.einsum(
        "td,sdk->tsk", normalized_rows, projected_lowrank_left, preferred_element_type=jnp.float32
    )
    seat_here = token_adapter_slot[:, None] == local_seats[None, :]
    lowrank_source = jnp.sum(jnp.where(seat_here[:, :, None], seat_factors, 0.0), axis=1)
    lowrank_source = sum_mp(lowrank_source).astype(jnp.bfloat16)
    choice_mask_table = membership.astype(jnp.bfloat16)
    broadened_lines = (choice_mask_table[:, :, None] * lowrank_source[:, None, :]).reshape(
        prompt_ordinal, SHARD_PROMPTS * LOW_DIMENSION
    )
    raised_result_lines = projected_lowrank_right[request_ids].reshape(
        SHARD_PROMPTS * LOW_DIMENSION, 3 * channel_window * CHANNEL_LENGTH
    )
    adapter_query_key_value = jnp.dot(
        broadened_lines, raised_result_lines, preferred_element_type=jnp.float32
    ).reshape(prompt_ordinal, 3, channel_window, CHANNEL_LENGTH)
    token_positions = positions_of(segments)
    rotary_queries = apply_rotary(
        query_rows + adapter_query_key_value[:, 0], token_positions
    ).astype(jnp.bfloat16)
    rotary_keys = apply_rotary(
        key_value_rows[:, 0] + adapter_query_key_value[:, 1], token_positions
    ).astype(jnp.bfloat16)
    fresh_values = (key_value_rows[:, 1] + adapter_query_key_value[:, 2]).astype(jnp.bfloat16)
    kv_new = jnp.stack([rotary_keys, fresh_values], axis=1)
    own_pages = lax.dynamic_index_in_dim(request_pages, dp_index, 0, keepdims=False).reshape(
        SHARD_PROMPTS * PPR
    )
    whole_pool = lax.all_gather(key_value_cache, DP_AXES, axis=0, tiled=True)
    chosen = whole_pool[own_pages]
    keys_pre = jnp.transpose(chosen[:, 0], (1, 0, 2, 3)).reshape(
        channel_window, SHARD_PROMPTS * PPR * PAGE, CHANNEL_LENGTH
    )
    values_pre = jnp.transpose(chosen[:, 1], (1, 0, 2, 3)).reshape(
        channel_window, SHARD_PROMPTS * PPR * PAGE, CHANNEL_LENGTH
    )
    attended = attend_local(
        rotary_queries, rotary_keys, fresh_values, keys_pre, values_pre, segments
    )
    request_output_down = result_lowrank_left[request_ids]
    request_output_factors = jnp.einsum(
        "tc,rck->trk", attended, request_output_down, preferred_element_type=jnp.float32
    )
    output_adapter_piece = jnp.sum(
        jnp.where(membership[:, :, None], request_output_factors, 0.0), axis=1
    )
    result_lowrank_source = sum_mp(output_adapter_piece).astype(jnp.bfloat16)
    result_seat_lines = result_lowrank_right.shape[0]
    output_slots = mp_index * result_seat_lines + jnp.arange(result_seat_lines, dtype=jnp.int32)
    resident_here = (token_adapter_slot[:, None] == output_slots[None, :]).astype(jnp.bfloat16)
    broadened_result = (resident_here[:, :, None] * result_lowrank_source[:, None, :]).reshape(
        prompt_ordinal, result_seat_lines * LOW_DIMENSION
    )
    raised_window = result_lowrank_right.reshape(result_seat_lines * LOW_DIMENSION, HIDDEN_BREADTH)
    attn_sum = scatter_mp(
        (
            jnp.dot(attended, output_weight, preferred_element_type=jnp.float32)
            + jnp.dot(broadened_result, raised_window, preferred_element_type=jnp.float32)
        ).astype(jnp.bfloat16)
    ).astype(jnp.float32)
    after_attn = (residual + rms_scale(attn_sum, after_attention_gain)).astype(jnp.bfloat16)
    normed_ffw = rms_scale(after_attn.astype(jnp.float32), before_feedforward_gain).astype(
        jnp.bfloat16
    )
    piece = gather_mp(normed_ffw)
    gated = jnp.dot(piece, gate_matrix, preferred_element_type=jnp.float32)
    upward = jnp.dot(piece, up_matrix, preferred_element_type=jnp.float32)
    hidden = (jax.nn.gelu(gated, approximate=True) * upward).astype(jnp.bfloat16)
    ffw_sum = scatter_mp(
        jnp.dot(hidden, down_matrix, preferred_element_type=jnp.float32).astype(jnp.bfloat16)
    ).astype(jnp.float32)
    hidden_out = (
        after_attn.astype(jnp.float32) + rms_scale(ffw_sum, after_feedforward_gain)
    ).astype(jnp.bfloat16)
    return (hidden_out, kv_new)


def solution(mesh):
    fine_mesh = jax.sharding.Mesh(
        mesh.devices.reshape(2, 2, 4, 4, 2), DP_AXES + MP_AXES
    )
    return jax.shard_map(
        shards,
        mesh=fine_mesh,
        in_specs=(
            P(DP_AXES + MP_AXES, None),
            P(),
            P(),
            P(),
            P(),
            P(None, MP_AXES),
            P(None, None, MP_AXES, None),
            P(MP_AXES, None),
            P(None, MP_AXES),
            P(None, MP_AXES),
            P(MP_AXES, None),
            P(DP_AXES, None, MP_AXES, None, None),
            P(MP_AXES, None, None),
            P(None, None, None, MP_AXES, None),
            P(None, MP_AXES, None),
            P(MP_AXES, None, None),
            P(DP_AXES, None),
            P(DP_AXES, None),
            P(),
            P(),
        ),
        out_specs=(P(DP_AXES + MP_AXES, None), P(DP_AXES, None, MP_AXES, None)),
        check_vma=False,
    )
```
